512 devices in a mesh: rows: 128 (over y_hi, x, z), rep: 4 (over y_lo, core).
Axes of the slice: x: 4, y: 8 (y_hi: 4, y_lo: 2; y = y_hi * 2 + y_lo), z: 8, core: 2. Of those that a mesh axis runs over, the one named last changes fastest.
Arguments:
- features: bfloat16 [65536, 256], P(('rows', 'rep')), may hold values from -6 to 6
- weight: bfloat16 [256, 256], replicated, may hold values from -0.375 to 0.375
- bias_terms: float32 [256], replicated, may hold values from -3 to 3
- tile_data: bfloat16 [128, 4, 8, 128, 128], P('rows'), may hold values from -0.1875 to 0.1875
- tile_row: int32 [128, 4, 8], P('rows'), may hold values from 0 to 3
- tile_col: int32 [128, 4, 8], P('rows'), may hold values from 0 to 127
- tile_count: int32 [128, 4], P('rows'), may hold values from 1 to 8, as said below
- grad_out: bfloat16 [65536, 256], P(('rows', 'rep')), may hold values from -6 to 6
Outputs:
- layer_out: bfloat16 [65536, 256], P(('rows', 'rep'))
- weight_grad: float32 [256, 256], replicated
- bias_grad: float32 [256], replicated
The draws below stay inside these ranges and needn't reach their ends.
Inputs may be any that keep to these rules, and one draw needn't show every extreme that they name: `tile_count`: some group's stripe has all 8 slots live in every draw.
All inputs are finite; a program needn't handle non-finite values.
Results may differ from the reference program's by a relative error of at most 0.015.
Values may be sent and summed in bfloat16 or wider, within the bound.
No kernel may reach another device: no remote copies, remote signals or barrier semaphores. Data moves between devices by JAX's collectives and lax.ppermute only.
A program may use at most 64 MiB of HBM per device.

```python
import jax
import jax.numpy as jnp
from jax import lax

F = 256
BLOCK = 128
CAP = 8
NBLK = 512
NODES = 65536
N_ROWS = 128
N_REP = 4


def draw_tile_count(key, part):
    first_key, second_key, third_key = jax.random.split(key, 3)
    base_counts = jax.random.randint(first_key, (N_ROWS, N_REP), 1, CAP // 2 + 1)
    full_flags = jax.random.randint(second_key, (N_ROWS, N_REP), 0, 8) == 0
    counts = jnp.where(full_flags, CAP, base_counts)
    spot = jax.random.randint(third_key, (), 0, N_ROWS * N_REP)
    flat_counts = counts.reshape(-1).at[spot].set(CAP)
    return flat_counts.reshape(N_ROWS, N_REP).astype(jnp.int32)


def plant(result, key, least, top_value):
    extent = result.shape
    index_at = [jax.random.randint(jax.random.fold_in(key, axis), (), 0, extent[axis]) for axis in range(len(extent))]
    result = result.at[tuple(index_at)].set(least)
    longest = extent.index(max(extent))
    index_at[longest] = (index_at[longest] + 1) % extent[longest]
    return result.at[tuple(index_at)].set(top_value)


def level_of(rng, extent, shards, least, top_value):
    gain, own = 1.0, jax.random.fold_in(rng, 6)
    for position, shards_of in shards:
        heights = jnp.exp(jax.random.uniform(jax.random.fold_in(own, position), (shards_of,), jnp.float32, least / len(shards), top_value / len(shards)))
        gain = gain * jnp.repeat(heights, extent[position] // shards_of).reshape([-1 if axis == position else 1 for axis in range(len(extent))])
    return gain


def normal_values(rng, shape, scale, reach, cuts=(), kind=jnp.bfloat16):
    drawn = scale * jax.random.normal(rng, shape, jnp.float32)
    if cuts:
        drawn = drawn * level_of(rng, shape, cuts, -0.22, 0.18)
    return jnp.clip(drawn, -reach, reach).astype(kind)


def setup_inputs(seed: int = 0) -> dict:
    arg_keys = jax.random.split(jax.random.key(seed), 9)
    return {
        "features": normal_values(arg_keys[0], (NODES, F), 1.0, 6.0, ((0, 512),)),
        "weight": normal_values(arg_keys[1], (F, F), F ** -0.5, 0.375),
        "bias_terms": normal_values(arg_keys[2], (F,), 0.5, 3.0, (), jnp.float32),
        "tile_data": normal_values(arg_keys[3], (N_ROWS, N_REP, CAP, BLOCK, BLOCK), (BLOCK * CAP) ** -0.5, 0.1875, ((0, 128),)),
        "tile_row": plant(jax.random.randint(arg_keys[4], (N_ROWS, N_REP, CAP), 0, N_REP), jax.random.fold_in(arg_keys[4], 1), 0, N_REP - 1).astype(jnp.int32),
        "tile_col": plant(jax.random.randint(arg_keys[5], (N_ROWS, N_REP, CAP), 0, N_ROWS), jax.random.fold_in(arg_keys[5], 1), 0, N_ROWS - 1).astype(jnp.int32),
        "tile_count": draw_tile_count(jax.random.fold_in(arg_keys[8], 71), 0),
        "grad_out": normal_values(arg_keys[7], (NODES, F), 1.0, 6.0, ((0, 512),)),
    }


def reference(features, weight, bias_terms, tile_data, tile_row, tile_col, tile_count, grad_out):
    blocks_all = features.reshape(NBLK, BLOCK, F)
    stripe_ids = jnp.arange(N_REP, dtype=jnp.int32)
    slot_ids = jnp.arange(CAP, dtype=jnp.int32)

    def one_group(packed):
        tile_grp, row_grp, col_grp, count_grp = packed
        global_col = (col_grp * N_REP + stripe_ids[:, None]).astype(jnp.int32)
        picked = blocks_all[global_col.reshape(-1)].astype(jnp.float32)
        product = jnp.einsum("tij,tjf->tif", tile_grp.reshape(-1, BLOCK, BLOCK).astype(jnp.float32), picked)
        live = (slot_ids[None, :] < count_grp[:, None]).reshape(-1)
        select = ((row_grp.reshape(-1)[None, :] == stripe_ids[:, None]) & live[None, :]).astype(jnp.float32)
        return jnp.einsum("bt,tif->bif", select, product)

    summed = lax.map(one_group, (tile_data, tile_row, tile_col, tile_count))
    propagated = summed.reshape(NODES, F).astype(jnp.bfloat16)
    preact = jnp.dot(propagated, weight, preferred_element_type=jnp.float32) + bias_terms
    sig = jax.nn.sigmoid(preact)
    layer_out = (preact * sig).astype(jnp.bfloat16)
    slope = sig * (1.0 + preact * (1.0 - sig))
    grad_pre = (grad_out.astype(jnp.float32) * slope).astype(jnp.bfloat16)
    weight_grad = jnp.dot(propagated.T, grad_pre, preferred_element_type=jnp.float32)
    bias_grad = jnp.sum(grad_pre.astype(jnp.float32), axis=0)
    return layer_out, weight_grad, bias_grad
```

```python
import jax
import jax.numpy as jnp
from jax import lax
from jax.sharding import Mesh
from jax.sharding import PartitionSpec as P

ROW_AXES = ("y_hi", "x", "z")
REP_AXES = ("y_lo", "core")
ALL_AXES = ROW_AXES + REP_AXES


def physical_mesh(mesh):
    rows, rep = mesh.devices.shape
    y_hi, x, y_lo = 4, 4, 2
    return Mesh(mesh.devices.reshape(y_hi, x, rows // (y_hi * x), y_lo, rep // y_lo), ALL_AXES)


def ring_gather(piece, axis):
    n = lax.axis_size(axis)
    fwd = [(i, (i + 1) % n) for i in range(n)]
    bwd = [(i, (i - 1) % n) for i in range(n)]
    pieces = {0: piece}
    left = piece
    right = piece
    for k in range(1, n // 2 + 1):
        left = lax.ppermute(left, axis, fwd)
        pieces[-k] = left
        if k < n - k:
            right = lax.ppermute(right, axis, bwd)
            pieces[k] = right
    return jnp.stack([pieces[d] for d in range(-(n // 2), n - n // 2)])


def gather_blocks(features, cols):
    order = ("y_hi", "x", "z")
    stack = features
    for a in order:
        stack = ring_gather(stack, a)
    blocks = stack.reshape(-1, features.shape[0], features.shape[1])
    return jnp.take(blocks, nested_slot(cols, order), axis=0)


def nested_slot(cols, order):
    sizes = {a: lax.axis_size(a) for a in ROW_AXES}
    coords = {}
    rest = cols
    for a in reversed(ROW_AXES):
        coords[a] = rest % sizes[a]
        rest = rest // sizes[a]
    flat = jnp.zeros_like(cols)
    for a in reversed(order):
        k = (coords[a] - lax.axis_index(a) + sizes[a] // 2) % sizes[a]
        flat = flat * sizes[a] + k
    return flat


def halving_steps(axes):
    steps = []
    for a in axes:
        n = lax.axis_size(a)
        for b in reversed(range(n.bit_length() - 1)):
            steps.append((a, b, [(i, i ^ (1 << b)) for i in range(n)]))
    return steps


def reduce_scatter_flat(flat, steps):
    for a, b, perm in steps:
        upper = (lax.axis_index(a) >> b) & 1
        half = flat.shape[0] // 2
        lower_half, upper_half = flat[:half], flat[half:]
        send = jnp.where(upper == 1, lower_half, upper_half)
        keep = jnp.where(upper == 1, upper_half, lower_half)
        flat = keep + lax.ppermute(send, a, perm)
    return flat


def all_gather_flat(flat, steps):
    for a, b, perm in reversed(steps):
        upper = (lax.axis_index(a) >> b) & 1
        other = lax.ppermute(flat, a, perm)
        flat = jnp.where(
            upper == 1, jnp.concatenate([other, flat]), jnp.concatenate([flat, other])
        )
    return flat


def reduce_all(packed):
    for a, b, perm in halving_steps(("core", "y_lo", "z", "x", "y_hi")):
        packed = packed + lax.ppermute(packed, a, perm)
    return packed


def reduce_over_rep(partial_value):
    steps = halving_steps(("y_lo", "core"))
    rows, width = partial_value.shape
    flat = reduce_scatter_flat(partial_value.reshape(-1), steps)
    return flat.reshape(rows // lax.axis_size(REP_AXES), width)


def shards(features, weight, bias_terms, tile_data, tile_row, tile_col, tile_count, grad_out):
    block_size = tile_data.shape[-1]
    feature_width = features.shape[1]
    row_count = lax.axis_size(REP_AXES)
    rep_index = lax.axis_index(REP_AXES)
    own_tiles = lax.dynamic_index_in_dim(tile_data[0], rep_index, 0, keepdims=False)
    own_rows = lax.dynamic_index_in_dim(tile_row[0], rep_index, 0, keepdims=False)
    own_cols = lax.dynamic_index_in_dim(tile_col[0], rep_index, 0, keepdims=False)
    own_count = lax.dynamic_index_in_dim(tile_count[0], rep_index, 0, keepdims=False)
    capacity = own_rows.shape[0]
    stripe_nodes = lax.all_gather(features, ROW_AXES, axis=0, tiled=True)
    picked = jnp.take(stripe_nodes.reshape(-1, block_size, feature_width), own_cols, axis=0)
    product = jnp.einsum("tij,tjf->tif", own_tiles, picked, preferred_element_type=jnp.float32)
    live = jnp.arange(capacity, dtype=jnp.int32) < own_count
    local_ids = jnp.arange(row_count, dtype=jnp.int32)
    select = ((own_rows[None, :] == local_ids[:, None]) & live[None, :]).astype(jnp.float32)
    partial_value = jnp.einsum("bt,tif->bif", select, product)
    partial_value = partial_value.reshape(row_count * block_size, feature_width)
    propagated = lax.psum_scatter(partial_value, REP_AXES, scatter_dimension=0, tiled=True).astype(
        jnp.bfloat16
    )
    preact = jnp.dot(propagated, weight, preferred_element_type=jnp.float32) + bias_terms
    sigma = jax.nn.sigmoid(preact)
    layer_out = (preact * sigma).astype(jnp.bfloat16)
    slope = sigma * (1.0 + preact * (1.0 - sigma))
    grad_pre = (grad_out.astype(jnp.float32) * slope).astype(jnp.bfloat16)
    weight_term = lax.dot_general(
        propagated, grad_pre, (((0,), (0,)), ((), ())), preferred_element_type=jnp.float32
    )
    bias_term = jnp.sum(grad_pre.astype(jnp.float32), axis=0)
    pad_rows = (-(feature_width + 1)) % 8
    packed = jnp.concatenate(
        [weight_term, bias_term[None, :], jnp.zeros((pad_rows, feature_width), jnp.float32)], axis=0
    )
    packed = reduce_all(packed)
    weight_grad = packed[:feature_width]
    bias_grad = packed[feature_width]
    return (layer_out, weight_grad, bias_grad)


def solution(mesh):
    flat = P(ALL_AXES, None)
    placed = (
        flat,
        P(),
        P(),
        P(ROW_AXES, None, None, None, None),
        P(ROW_AXES, None, None),
        P(ROW_AXES, None, None),
        P(ROW_AXES, None),
        flat,
    )
    return jax.shard_map(
        shards,
        mesh=physical_mesh(mesh),
        in_specs=placed,
        out_specs=(flat, P(), P()),
        check_vma=False,
    )
```

```python
import jax
import jax.numpy as jnp
from jax import lax
from jax.sharding import Mesh
from jax.sharding import PartitionSpec as P

ROW_AXES = ("y_hi", "x", "z")
REP_AXES = ("y_lo", "core")
ALL_AXES = ROW_AXES + REP_AXES
SPLIT = 64


def physical_mesh(mesh):
    rows, rep = mesh.devices.shape
    y_hi, x, y_lo = 4, 4, 2
    return Mesh(mesh.devices.reshape(y_hi, x, rows // (y_hi * x), y_lo, rep // y_lo), ALL_AXES)


def ring_gather(piece, axis):
    n = lax.axis_size(axis)
    fwd = [(i, (i + 1) % n) for i in range(n)]
    bwd = [(i, (i - 1) % n) for i in range(n)]
    pieces = {0: piece}
    left = piece
    right = piece
    for k in range(1, n // 2 + 1):
        left = lax.ppermute(left, axis, fwd)
        pieces[-k] = left
        if k < n - k:
            right = lax.ppermute(right, axis, bwd)
            pieces[k] = right
    return jnp.stack([pieces[d] for d in range(-(n // 2), n - n // 2)])


def ring_blocks(features, cols, order):
    stack = features
    for a in order:
        stack = ring_gather(stack, a)
    blocks = stack.reshape(-1, features.shape[0], features.shape[1])
    return jnp.take(blocks, nested_slot(cols, order), axis=0)


def nested_slot(cols, order):
    sizes = {a: lax.axis_size(a) for a in ROW_AXES}
    coords = {}
    rest = cols
    for a in reversed(ROW_AXES):
        coords[a] = rest % sizes[a]
        rest = rest // sizes[a]
    flat = jnp.zeros_like(cols)
    for a in reversed(order):
        k = (coords[a] - lax.axis_index(a) + sizes[a] // 2) % sizes[a]
        flat = flat * sizes[a] + k
    return flat


def halving_steps(axes):
    steps = []
    for a in axes:
        n = lax.axis_size(a)
        for b in reversed(range(n.bit_length() - 1)):
            steps.append((a, b, [(i, i ^ (1 << b)) for i in range(n)]))
    return steps


def reduce_scatter_flat(flat, steps):
    for a, b, perm in steps:
        upper = (lax.axis_index(a) >> b) & 1
        half = flat.shape[0] // 2
        lower_half, upper_half = flat[:half], flat[half:]
        send = jnp.where(upper == 1, lower_half, upper_half)
        keep = jnp.where(upper == 1, upper_half, lower_half)
        flat = keep + lax.ppermute(send, a, perm)
    return flat


def all_gather_flat(flat, steps):
    for a, b, perm in reversed(steps):
        upper = (lax.axis_index(a) >> b) & 1
        other = lax.ppermute(flat, a, perm)
        flat = jnp.where(
            upper == 1, jnp.concatenate([other, flat]), jnp.concatenate([flat, other])
        )
    return flat


def reduce_all(packed):
    for a, b, perm in halving_steps(("core", "y_lo", "z", "x", "y_hi")):
        packed = packed + lax.ppermute(packed, a, perm)
    return packed


def reduce_over_rep(partial_value):
    steps = halving_steps(("y_lo", "core"))
    rows, width = partial_value.shape
    flat = reduce_scatter_flat(partial_value.reshape(-1), steps)
    return flat.reshape(rows // lax.axis_size(REP_AXES), width)


def shards(features, weight, bias_terms, tile_data, tile_row, tile_col, tile_count, grad_out):
    block_size = tile_data.shape[-1]
    feature_width = features.shape[1]
    row_count = lax.axis_size(REP_AXES)
    rep_index = lax.axis_index(REP_AXES)
    own_tiles = lax.dynamic_index_in_dim(tile_data[0], rep_index, 0, keepdims=False)
    own_rows = lax.dynamic_index_in_dim(tile_row[0], rep_index, 0, keepdims=False)
    own_cols = lax.dynamic_index_in_dim(tile_col[0], rep_index, 0, keepdims=False)
    own_count = lax.dynamic_index_in_dim(tile_count[0], rep_index, 0, keepdims=False)
    capacity = own_rows.shape[0]
    near = features[:SPLIT]
    far = features[SPLIT:]
    stripe_nodes = lax.all_gather(near, ROW_AXES, axis=0, tiled=True)
    picked_near = jnp.take(stripe_nodes.reshape(-1, SPLIT, feature_width), own_cols, axis=0)
    picked_far = ring_blocks(far, own_cols, ("y_hi", "z", "x"))
    picked = jnp.concatenate([picked_near, picked_far], axis=1)
    product = jnp.einsum("tij,tjf->tif", own_tiles, picked, preferred_element_type=jnp.float32)
    live = jnp.arange(capacity, dtype=jnp.int32) < own_count
    local_ids = jnp.arange(row_count, dtype=jnp.int32)
    select = ((own_rows[None, :] == local_ids[:, None]) & live[None, :]).astype(jnp.float32)
    partial_value = jnp.einsum("bt,tif->bif", select, product)
    partial_value = partial_value.reshape(row_count * block_size, feature_width)
    propagated = lax.psum_scatter(partial_value, REP_AXES, scatter_dimension=0, tiled=True).astype(
        jnp.bfloat16
    )
    preact = jnp.dot(propagated, weight, preferred_element_type=jnp.float32) + bias_terms
    sigma = jax.nn.sigmoid(preact)
    layer_out = (preact * sigma).astype(jnp.bfloat16)
    slope = sigma * (1.0 + preact * (1.0 - sigma))
    grad_pre = (grad_out.astype(jnp.float32) * slope).astype(jnp.bfloat16)
    weight_term = lax.dot_general(
        propagated, grad_pre, (((0,), (0,)), ((), ())), preferred_element_type=jnp.float32
    )
    bias_term = jnp.sum(grad_pre.astype(jnp.float32), axis=0)
    pad_rows = (-(feature_width + 1)) % 8
    packed = jnp.concatenate(
        [weight_term, bias_term[None, :], jnp.zeros((pad_rows, feature_width), jnp.float32)], axis=0
    )
    packed = reduce_all(packed)
    weight_grad = packed[:feature_width]
    bias_grad = packed[feature_width]
    return (layer_out, weight_grad, bias_grad)


def solution(mesh):
    flat = P(ALL_AXES, None)
    placed = (
        flat,
        P(),
        P(),
        P(ROW_AXES, None, None, None, None),
        P(ROW_AXES, None, None),
        P(ROW_AXES, None, None),
        P(ROW_AXES, None),
        flat,
    )
    return jax.shard_map(
        shards,
        mesh=physical_mesh(mesh),
        in_specs=placed,
        out_specs=(flat, P(), P()),
        check_vma=False,
    )
```

```python
import jax
import jax.numpy as jnp
from jax import lax
from jax.sharding import Mesh
from jax.sharding import PartitionSpec as P

ROW_AXES = ("y_hi", "x", "z")
REP_AXES = ("y_lo", "core")
ALL_AXES = ROW_AXES + REP_AXES
SPLIT = 64


def physical_mesh(mesh):
    rows, rep = mesh.devices.shape
    y_hi, x, y_lo = 4, 4, 2
    return Mesh(mesh.devices.reshape(y_hi, x, rows // (y_hi * x), y_lo, rep // y_lo), ALL_AXES)


def ring_gather(piece, axis):
    n = lax.axis_size(axis)
    fwd = [(i, (i + 1) % n) for i in range(n)]
    bwd = [(i, (i - 1) % n) for i in range(n)]
    pieces = {0: piece}
    left = piece
    right = piece
    for k in range(1, n // 2 + 1):
        left = lax.ppermute(left, axis, fwd)
        pieces[-k] = left
        if k < n - k:
            right = lax.ppermute(right, axis, bwd)
            pieces[k] = right
    return jnp.stack([pieces[d] for d in range(-(n // 2), n - n // 2)])


def ring_blocks(features, cols, order):
    stack = features
    for a in order:
        stack = ring_gather(stack, a)
    blocks = stack.reshape(-1, features.shape[0], features.shape[1])
    return jnp.take(blocks, nested_slot(cols, order), axis=0)


def nested_slot(cols, order):
    sizes = {a: lax.axis_size(a) for a in ROW_AXES}
    coords = {}
    rest = cols
    for a in reversed(ROW_AXES):
        coords[a] = rest % sizes[a]
        rest = rest // sizes[a]
    flat = jnp.zeros_like(cols)
    for a in reversed(order):
        k = (coords[a] - lax.axis_index(a) + sizes[a] // 2) % sizes[a]
        flat = flat * sizes[a] + k
    return flat


def halving_steps(axes):
    steps = []
    for a in axes:
        n = lax.axis_size(a)
        for b in reversed(range(n.bit_length() - 1)):
            steps.append((a, b, [(i, i ^ (1 << b)) for i in range(n)]))
    return steps


def reduce_scatter_flat(flat, steps):
    for a, b, perm in steps:
        upper = (lax.axis_index(a) >> b) & 1
        half = flat.shape[0] // 2
        lower_half, upper_half = flat[:half], flat[half:]
        send = jnp.where(upper == 1, lower_half, upper_half)
        keep = jnp.where(upper == 1, upper_half, lower_half)
        flat = keep + lax.ppermute(send, a, perm)
    return flat


def all_gather_flat(flat, steps):
    for a, b, perm in reversed(steps):
        upper = (lax.axis_index(a) >> b) & 1
        other = lax.ppermute(flat, a, perm)
        flat = jnp.where(
            upper == 1, jnp.concatenate([other, flat]), jnp.concatenate([flat, other])
        )
    return flat


def reduce_all(packed):
    rep_steps = halving_steps(("core", "y_lo"))
    flat = reduce_scatter_flat(packed.reshape(-1), rep_steps)
    for a, b, perm in halving_steps(ROW_AXES[::-1]):
        flat = flat + lax.ppermute(flat, a, perm)
    flat = all_gather_flat(flat, rep_steps)
    return flat.reshape(packed.shape)


def reduce_over_rep(partial_value):
    rows, width = partial_value.shape
    blocks = partial_value.reshape(lax.axis_size("y_lo"), lax.axis_size("core"), -1)
    core = lax.axis_index("core")
    send = jnp.where(core == 1, blocks[:, 0], blocks[:, 1])
    keep = jnp.where(core == 1, blocks[:, 1], blocks[:, 0])
    pairs = keep + lax.ppermute(send, "core", [(0, 1), (1, 0)])
    y_lo = lax.axis_index("y_lo")
    send = jnp.where(y_lo == 1, pairs[0], pairs[1])
    keep = jnp.where(y_lo == 1, pairs[1], pairs[0])
    own = keep + lax.ppermute(send, "y_lo", [(0, 1), (1, 0)])
    return own.reshape(rows // lax.axis_size(REP_AXES), width)


def shards(features, weight, bias_terms, tile_data, tile_row, tile_col, tile_count, grad_out):
    block_size = tile_data.shape[-1]
    feature_width = features.shape[1]
    row_count = lax.axis_size(REP_AXES)
    rep_index = lax.axis_index(REP_AXES)
    own_tiles = lax.dynamic_index_in_dim(tile_data[0], rep_index, 0, keepdims=False)
    own_rows = lax.dynamic_index_in_dim(tile_row[0], rep_index, 0, keepdims=False)
    own_cols = lax.dynamic_index_in_dim(tile_col[0], rep_index, 0, keepdims=False)
    own_count = lax.dynamic_index_in_dim(tile_count[0], rep_index, 0, keepdims=False)
    capacity = own_rows.shape[0]
    near = features[:SPLIT]
    far = features[SPLIT:]
    stripe_nodes = lax.all_gather(near, ROW_AXES, axis=0, tiled=True)
    picked_near = jnp.take(stripe_nodes.reshape(-1, SPLIT, feature_width), own_cols, axis=0)
    picked_far = ring_blocks(far, own_cols, ("y_hi", "z", "x"))
    picked = jnp.concatenate([picked_near, picked_far], axis=1)
    product = jnp.einsum("tij,tjf->tif", own_tiles, picked, preferred_element_type=jnp.float32)
    live = jnp.arange(capacity, dtype=jnp.int32) < own_count
    local_ids = jnp.arange(row_count, dtype=jnp.int32)
    select = ((own_rows[None, :] == local_ids[:, None]) & live[None, :]).astype(jnp.float32)
    partial_value = jnp.einsum("bt,tif->bif", select, product)
    partial_value = partial_value.reshape(row_count * block_size, feature_width)
    propagated = reduce_over_rep(partial_value).astype(jnp.bfloat16)
    preact = jnp.dot(propagated, weight, preferred_element_type=jnp.float32) + bias_terms
    sigma = jax.nn.sigmoid(preact)
    layer_out = (preact * sigma).astype(jnp.bfloat16)
    slope = sigma * (1.0 + preact * (1.0 - sigma))
    grad_pre = (grad_out.astype(jnp.float32) * slope).astype(jnp.bfloat16)
    weight_term = lax.dot_general(
        propagated, grad_pre, (((0,), (0,)), ((), ())), preferred_element_type=jnp.float32
    )
    bias_term = jnp.sum(grad_pre.astype(jnp.float32), axis=0)
    pad_rows = (-(feature_width + 1)) % 8
    packed = jnp.concatenate(
        [weight_term, bias_term[None, :], jnp.zeros((pad_rows, feature_width), jnp.float32)], axis=0
    )
    packed = reduce_all(packed)
    weight_grad = packed[:feature_width]
    bias_grad = packed[feature_width]
    return (layer_out, weight_grad, bias_grad)


def solution(mesh):
    flat = P(ALL_AXES, None)
    placed = (
        flat,
        P(),
        P(),
        P(ROW_AXES, None, None, None, None),
        P(ROW_AXES, None, None),
        P(ROW_AXES, None, None),
        P(ROW_AXES, None),
        flat,
    )
    return jax.shard_map(
        shards,
        mesh=physical_mesh(mesh),
        in_specs=placed,
        out_specs=(flat, P(), P()),
        check_vma=False,
    )
```

```python
import jax
import jax.numpy as jnp
from jax import lax
from jax.sharding import Mesh
from jax.sharding import PartitionSpec as P

ROW_AXES = ("y_hi", "x", "z")
REP_AXES = ("y_lo", "core")
ALL_AXES = ROW_AXES + REP_AXES
SPLIT = 64


def physical_mesh(mesh):
    rows, rep = mesh.devices.shape
    y_hi, x, y_lo = 4, 4, 2
    return Mesh(mesh.devices.reshape(y_hi, x, rows // (y_hi * x), y_lo, rep // y_lo), ALL_AXES)


def ring_gather(piece, axis):
    n = lax.axis_size(axis)
    fwd = [(i, (i + 1) % n) for i in range(n)]
    bwd = [(i, (i - 1) % n) for i in range(n)]
    pieces = {0: piece}
    left = piece
    right = piece
    for k in range(1, n // 2 + 1):
        left = lax.ppermute(left, axis, fwd)
        pieces[-k] = left
        if k < n - k:
            right = lax.ppermute(right, axis, bwd)
            pieces[k] = right
    return jnp.stack([pieces[d] for d in range(-(n // 2), n - n // 2)])


def ring_blocks(features, cols, order):
    stack = features
    for a in order:
        stack = ring_gather(stack, a)
    blocks = stack.reshape(-1, features.shape[0], features.shape[1])
    return jnp.take(blocks, nested_slot(cols, order), axis=0)


def nested_slot(cols, order):
    sizes = {a: lax.axis_size(a) for a in ROW_AXES}
    coords = {}
    rest = cols
    for a in reversed(ROW_AXES):
        coords[a] = rest % sizes[a]
        rest = rest // sizes[a]
    flat = jnp.zeros_like(cols)
    for a in reversed(order):
        k = (coords[a] - lax.axis_index(a) + sizes[a] // 2) % sizes[a]
        flat = flat * sizes[a] + k
    return flat


def halving_steps(axes):
    steps = []
    for a in axes:
        n = lax.axis_size(a)
        for b in reversed(range(n.bit_length() - 1)):
            steps.append((a, b, [(i, i ^ (1 << b)) for i in range(n)]))
    return steps


def reduce_scatter_flat(flat, steps):
    for a, b, perm in steps:
        upper = (lax.axis_index(a) >> b) & 1
        half = flat.shape[0] // 2
        lower_half, upper_half = flat[:half], flat[half:]
        send = jnp.where(upper == 1, lower_half, upper_half)
        keep = jnp.where(upper == 1, upper_half, lower_half)
        flat = keep + lax.ppermute(send, a, perm)
    return flat


def all_gather_flat(flat, steps):
    for a, b, perm in reversed(steps):
        upper = (lax.axis_index(a) >> b) & 1
        other = lax.ppermute(flat, a, perm)
        flat = jnp.where(
            upper == 1, jnp.concatenate([other, flat]), jnp.concatenate([flat, other])
        )
    return flat


def reduce_all(packed):
    rep_steps = halving_steps(("core", "y_lo"))
    flat = reduce_scatter_flat(packed.reshape(-1), rep_steps)
    for a, b, perm in halving_steps(ROW_AXES[::-1]):
        flat = flat + lax.ppermute(flat, a, perm)
    flat = all_gather_flat(flat, rep_steps)
    return flat.reshape(packed.shape)


def reduce_over_rep(partial_value):
    rows, width = partial_value.shape
    blocks = partial_value.reshape(lax.axis_size("y_lo"), lax.axis_size("core"), -1)
    core = lax.axis_index("core")
    send = jnp.where(core == 1, blocks[:, 0], blocks[:, 1])
    keep = jnp.where(core == 1, blocks[:, 1], blocks[:, 0])
    pairs = keep + lax.ppermute(send, "core", [(0, 1), (1, 0)])
    y_lo = lax.axis_index("y_lo")
    send = jnp.where(y_lo == 1, pairs[0], pairs[1])
    keep = jnp.where(y_lo == 1, pairs[1], pairs[0])
    own = keep + lax.ppermute(send, "y_lo", [(0, 1), (1, 0)])
    return own.reshape(rows // lax.axis_size(REP_AXES), width)


def shards(features, weight, bias_terms, tile_data, tile_row, tile_col, tile_count, grad_out):
    block_size = tile_data.shape[-1]
    feature_width = features.shape[1]
    row_count = lax.axis_size(REP_AXES)
    rep_index = lax.axis_index(REP_AXES)
    own_tiles = lax.dynamic_index_in_dim(tile_data[0], rep_index, 0, keepdims=False)
    own_rows = lax.dynamic_index_in_dim(tile_row[0], rep_index, 0, keepdims=False)
    own_cols = lax.dynamic_index_in_dim(tile_col[0], rep_index, 0, keepdims=False)
    own_count = lax.dynamic_index_in_dim(tile_count[0], rep_index, 0, keepdims=False)
    capacity = own_rows.shape[0]
    picked_near = ring_blocks(features[:SPLIT], own_cols, ("y_hi", "x", "z"))
    picked_far = ring_blocks(features[SPLIT:], own_cols, ("y_hi", "z", "x"))
    picked = jnp.concatenate([picked_near, picked_far], axis=1)
    product = jnp.einsum("tij,tjf->tif", own_tiles, picked, preferred_element_type=jnp.float32)
    live = jnp.arange(capacity, dtype=jnp.int32) < own_count
    local_ids = jnp.arange(row_count, dtype=jnp.int32)
    select = ((own_rows[None, :] == local_ids[:, None]) & live[None, :]).astype(jnp.float32)
    partial_value = jnp.einsum("bt,tif->bif", select, product)
    partial_value = partial_value.reshape(row_count * block_size, feature_width)
    propagated = reduce_over_rep(partial_value).astype(jnp.bfloat16)
    preact = jnp.dot(propagated, weight, preferred_element_type=jnp.float32) + bias_terms
    sigma = jax.nn.sigmoid(preact)
    layer_out = (preact * sigma).astype(jnp.bfloat16)
    slope = sigma * (1.0 + preact * (1.0 - sigma))
    grad_pre = (grad_out.astype(jnp.float32) * slope).astype(jnp.bfloat16)
    weight_term = lax.dot_general(
        propagated, grad_pre, (((0,), (0,)), ((), ())), preferred_element_type=jnp.float32
    )
    bias_term = jnp.sum(grad_pre.astype(jnp.float32), axis=0)
    pad_rows = (-(feature_width + 1)) % 8
    packed = jnp.concatenate(
        [weight_term, bias_term[None, :], jnp.zeros((pad_rows, feature_width), jnp.float32)], axis=0
    )
    packed = reduce_all(packed)
    weight_grad = packed[:feature_width]
    bias_grad = packed[feature_width]
    return (layer_out, weight_grad, bias_grad)


def solution(mesh):
    flat = P(ALL_AXES, None)
    placed = (
        flat,
        P(),
        P(),
        P(ROW_AXES, None, None, None, None),
        P(ROW_AXES, None, None),
        P(ROW_AXES, None, None),
        P(ROW_AXES, None),
        flat,
    )
    return jax.shard_map(
        shards,
        mesh=physical_mesh(mesh),
        in_specs=placed,
        out_specs=(flat, P(), P()),
        check_vma=False,
    )
```

```python
import jax
import jax.numpy as jnp
from jax import lax
from jax.sharding import Mesh
from jax.sharding import PartitionSpec as P

ROW_AXES = ("y_hi", "x", "z")
REP_AXES = ("y_lo", "core")
ALL_AXES = ROW_AXES + REP_AXES


def physical_mesh(mesh):
    rows, rep = mesh.devices.shape
    y_hi, x, y_lo = 4, 4, 2
    return Mesh(mesh.devices.reshape(y_hi, x, rows // (y_hi * x), y_lo, rep // y_lo), ALL_AXES)


def ring_gather(piece, axis):
    n = lax.axis_size(axis)
    fwd = [(i, (i + 1) % n) for i in range(n)]
    bwd = [(i, (i - 1) % n) for i in range(n)]
    pieces = {0: piece}
    left = piece
    right = piece
    for k in range(1, n // 2 + 1):
        left = lax.ppermute(left, axis, fwd)
        pieces[-k] = left
        if k < n - k:
            right = lax.ppermute(right, axis, bwd)
            pieces[k] = right
    return jnp.stack([pieces[d] for d in range(-(n // 2), n - n // 2)])


def plane_blocks(features, cols):
    sizes = {a: lax.axis_size(a) for a in ROW_AXES}
    n_plane = sizes["y_hi"]
    peer_cols = {
        s: lax.ppermute(cols, "y_hi", [(i, (i - s) % n_plane) for i in range(n_plane)])
        for s in range(1, n_plane)
    }
    stack = features
    for a in ("z", "x"):
        stack = ring_gather(stack, a)
    plane = stack.reshape(-1, features.shape[0], features.shape[1])

    def in_plane(c):
        z = c % sizes["z"]
        x = (c // sizes["z"]) % sizes["x"]
        kz = (z - lax.axis_index("z") + sizes["z"] // 2) % sizes["z"]
        kx = (x - lax.axis_index("x") + sizes["x"] // 2) % sizes["x"]
        return kx * sizes["z"] + kz

    picked = jnp.take(plane, in_plane(cols), axis=0)
    source = (lax.axis_index("y_hi") - cols // (sizes["z"] * sizes["x"])) % n_plane
    for s in range(1, n_plane):
        sent = jnp.take(plane, in_plane(peer_cols[s]), axis=0)
        got = lax.ppermute(sent, "y_hi", [(i, (i + s) % n_plane) for i in range(n_plane)])
        picked = jnp.where((source == s)[:, None, None], got, picked)
    return picked


def halving_steps(axes):
    steps = []
    for a in axes:
        n = lax.axis_size(a)
        for b in reversed(range(n.bit_length() - 1)):
            steps.append((a, b, [(i, i ^ (1 << b)) for i in range(n)]))
    return steps


def reduce_scatter_flat(flat, steps):
    for a, b, perm in steps:
        upper = (lax.axis_index(a) >> b) & 1
        half = flat.shape[0] // 2
        lower_half, upper_half = flat[:half], flat[half:]
        send = jnp.where(upper == 1, lower_half, upper_half)
        keep = jnp.where(upper == 1, upper_half, lower_half)
        flat = keep + lax.ppermute(send, a, perm)
    return flat


def all_gather_flat(flat, steps):
    for a, b, perm in reversed(steps):
        upper = (lax.axis_index(a) >> b) & 1
        other = lax.ppermute(flat, a, perm)
        flat = jnp.where(
            upper == 1, jnp.concatenate([other, flat]), jnp.concatenate([flat, other])
        )
    return flat


def reduce_all(packed):
    rep_steps = halving_steps(("core", "y_lo"))
    flat = reduce_scatter_flat(packed.reshape(-1), rep_steps)
    for a, b, perm in halving_steps(ROW_AXES[::-1]):
        flat = flat + lax.ppermute(flat, a, perm)
    flat = all_gather_flat(flat, rep_steps)
    return flat.reshape(packed.shape)


def reduce_over_rep(partial_value):
    rows, width = partial_value.shape
    blocks = partial_value.reshape(lax.axis_size("y_lo"), lax.axis_size("core"), -1)
    core = lax.axis_index("core")
    send = jnp.where(core == 1, blocks[:, 0], blocks[:, 1])
    keep = jnp.where(core == 1, blocks[:, 1], blocks[:, 0])
    pairs = keep + lax.ppermute(send, "core", [(0, 1), (1, 0)])
    y_lo = lax.axis_index("y_lo")
    send = jnp.where(y_lo == 1, pairs[0], pairs[1])
    keep = jnp.where(y_lo == 1, pairs[1], pairs[0])
    own = keep + lax.ppermute(send, "y_lo", [(0, 1), (1, 0)])
    return own.reshape(rows // lax.axis_size(REP_AXES), width)


def shards(features, weight, bias_terms, tile_data, tile_row, tile_col, tile_count, grad_out):
    block_size = tile_data.shape[-1]
    feature_width = features.shape[1]
    row_count = lax.axis_size(REP_AXES)
    rep_index = lax.axis_index(REP_AXES)
    own_tiles = lax.dynamic_index_in_dim(tile_data[0], rep_index, 0, keepdims=False)
    own_rows = lax.dynamic_index_in_dim(tile_row[0], rep_index, 0, keepdims=False)
    own_cols = lax.dynamic_index_in_dim(tile_col[0], rep_index, 0, keepdims=False)
    own_count = lax.dynamic_index_in_dim(tile_count[0], rep_index, 0, keepdims=False)
    capacity = own_rows.shape[0]
    picked = plane_blocks(features, own_cols)
    product = jnp.einsum("tij,tjf->tif", own_tiles, picked, preferred_element_type=jnp.float32)
    live = jnp.arange(capacity, dtype=jnp.int32) < own_count
    local_ids = jnp.arange(row_count, dtype=jnp.int32)
    select = ((own_rows[None, :] == local_ids[:, None]) & live[None, :]).astype(jnp.float32)
    partial_value = jnp.einsum("bt,tif->bif", select, product)
    partial_value = partial_value.reshape(row_count * block_size, feature_width)
    propagated = reduce_over_rep(partial_value).astype(jnp.bfloat16)
    preact = jnp.dot(propagated, weight, preferred_element_type=jnp.float32) + bias_terms
    sigma = jax.nn.sigmoid(preact)
    layer_out = (preact * sigma).astype(jnp.bfloat16)
    slope = sigma * (1.0 + preact * (1.0 - sigma))
    grad_pre = (grad_out.astype(jnp.float32) * slope).astype(jnp.bfloat16)
    weight_term = lax.dot_general(
        propagated, grad_pre, (((0,), (0,)), ((), ())), preferred_element_type=jnp.float32
    )
    bias_term = jnp.sum(grad_pre.astype(jnp.float32), axis=0)
    pad_rows = (-(feature_width + 1)) % 8
    packed = jnp.concatenate(
        [weight_term, bias_term[None, :], jnp.zeros((pad_rows, feature_width), jnp.float32)], axis=0
    )
    packed = reduce_all(packed)
    weight_grad = packed[:feature_width]
    bias_grad = packed[feature_width]
    return (layer_out, weight_grad, bias_grad)


def solution(mesh):
    flat = P(ALL_AXES, None)
    placed = (
        flat,
        P(),
        P(),
        P(ROW_AXES, None, None, None, None),
        P(ROW_AXES, None, None),
        P(ROW_AXES, None, None),
        P(ROW_AXES, None),
        flat,
    )
    return jax.shard_map(
        shards,
        mesh=physical_mesh(mesh),
        in_specs=placed,
        out_specs=(flat, P(), P()),
        check_vma=False,
    )
```

```python
import jax
import jax.numpy as jnp
from jax import lax
from jax.sharding import Mesh
from jax.sharding import PartitionSpec as P

ROW_AXES = ("y_hi", "x", "z")
REP_AXES = ("y_lo", "core")
ALL_AXES = ROW_AXES + REP_AXES


def physical_mesh(mesh):
    rows, rep = mesh.devices.shape
    y_hi, x, y_lo = 4, 4, 2
    return Mesh(mesh.devices.reshape(y_hi, x, rows // (y_hi * x), y_lo, rep // y_lo), ALL_AXES)


def ring_gather(piece, axis):
    n = lax.axis_size(axis)
    fwd = [(i, (i + 1) % n) for i in range(n)]
    bwd = [(i, (i - 1) % n) for i in range(n)]
    pieces = {0: piece}
    left = piece
    right = piece
    for k in range(1, n // 2 + 1):
        left = lax.ppermute(left, axis, fwd)
        pieces[-k] = left
        if k < n - k:
            right = lax.ppermute(right, axis, bwd)
            pieces[k] = right
    return jnp.stack([pieces[d] for d in range(-(n // 2), n - n // 2)])


def row_coords(c):
    coords = {}
    for a in reversed(ROW_AXES):
        size = lax.axis_size(a)
        coords[a] = c % size
        c = c // size
    return coords


def plane_blocks(features, cols, across="x", within=("y_hi", "z")):
    n_across = lax.axis_size(across)
    peer_cols = {
        s: lax.ppermute(cols, across, [(i, (i - s) % n_across) for i in range(n_across)])
        for s in range(1, n_across)
    }
    stack = features
    for a in within:
        stack = ring_gather(stack, a)
    plane = stack.reshape(-1, features.shape[0], features.shape[1])

    def in_plane(c):
        coords = row_coords(c)
        flat = jnp.zeros_like(c)
        for a in reversed(within):
            size = lax.axis_size(a)
            flat = flat * size + (coords[a] - lax.axis_index(a) + size // 2) % size
        return flat

    picked = jnp.take(plane, in_plane(cols), axis=0)
    source = (lax.axis_index(across) - row_coords(cols)[across]) % n_across
    for s in range(1, n_across):
        sent = jnp.take(plane, in_plane(peer_cols[s]), axis=0)
        got = lax.ppermute(sent, across, [(i, (i + s) % n_across) for i in range(n_across)])
        picked = jnp.where((source == s)[:, None, None], got, picked)
    return picked


def halving_steps(axes):
    steps = []
    for a in axes:
        n = lax.axis_size(a)
        for b in reversed(range(n.bit_length() - 1)):
            steps.append((a, b, [(i, i ^ (1 << b)) for i in range(n)]))
    return steps


def reduce_scatter_flat(flat, steps):
    for a, b, perm in steps:
        upper = (lax.axis_index(a) >> b) & 1
        half = flat.shape[0] // 2
        lower_half, upper_half = flat[:half], flat[half:]
        send = jnp.where(upper == 1, lower_half, upper_half)
        keep = jnp.where(upper == 1, upper_half, lower_half)
        flat = keep + lax.ppermute(send, a, perm)
    return flat


def all_gather_flat(flat, steps):
    for a, b, perm in reversed(steps):
        upper = (lax.axis_index(a) >> b) & 1
        other = lax.ppermute(flat, a, perm)
        flat = jnp.where(
            upper == 1, jnp.concatenate([other, flat]), jnp.concatenate([flat, other])
        )
    return flat


def reduce_all(packed):
    rep_steps = halving_steps(("core", "y_lo"))
    flat = reduce_scatter_flat(packed.reshape(-1), rep_steps)
    for a, b, perm in halving_steps(ROW_AXES[::-1]):
        flat = flat + lax.ppermute(flat, a, perm)
    flat = all_gather_flat(flat, rep_steps)
    return flat.reshape(packed.shape)


def reduce_over_rep(partial_value):
    rows, width = partial_value.shape
    blocks = partial_value.reshape(lax.axis_size("y_lo"), lax.axis_size("core"), -1)
    core = lax.axis_index("core")
    send = jnp.where(core == 1, blocks[:, 0], blocks[:, 1])
    keep = jnp.where(core == 1, blocks[:, 1], blocks[:, 0])
    pairs = keep + lax.ppermute(send, "core", [(0, 1), (1, 0)])
    y_lo = lax.axis_index("y_lo")
    send = jnp.where(y_lo == 1, pairs[0], pairs[1])
    keep = jnp.where(y_lo == 1, pairs[1], pairs[0])
    own = keep + lax.ppermute(send, "y_lo", [(0, 1), (1, 0)])
    return own.reshape(rows // lax.axis_size(REP_AXES), width)


def shards(features, weight, bias_terms, tile_data, tile_row, tile_col, tile_count, grad_out):
    block_size = tile_data.shape[-1]
    feature_width = features.shape[1]
    row_count = lax.axis_size(REP_AXES)
    rep_index = lax.axis_index(REP_AXES)
    own_tiles = lax.dynamic_index_in_dim(tile_data[0], rep_index, 0, keepdims=False)
    own_rows = lax.dynamic_index_in_dim(tile_row[0], rep_index, 0, keepdims=False)
    own_cols = lax.dynamic_index_in_dim(tile_col[0], rep_index, 0, keepdims=False)
    own_count = lax.dynamic_index_in_dim(tile_count[0], rep_index, 0, keepdims=False)
    capacity = own_rows.shape[0]
    picked = plane_blocks(features, own_cols)
    product = jnp.einsum("tij,tjf->tif", own_tiles, picked, preferred_element_type=jnp.float32)
    live = jnp.arange(capacity, dtype=jnp.int32) < own_count
    local_ids = jnp.arange(row_count, dtype=jnp.int32)
    select = ((own_rows[None, :] == local_ids[:, None]) & live[None, :]).astype(jnp.float32)
    partial_value = jnp.einsum("bt,tif->bif", select, product)
    partial_value = partial_value.reshape(row_count * block_size, feature_width)
    propagated = reduce_over_rep(partial_value).astype(jnp.bfloat16)
    preact = jnp.dot(propagated, weight, preferred_element_type=jnp.float32) + bias_terms
    sigma = jax.nn.sigmoid(preact)
    layer_out = (preact * sigma).astype(jnp.bfloat16)
    slope = sigma * (1.0 + preact * (1.0 - sigma))
    grad_pre = (grad_out.astype(jnp.float32) * slope).astype(jnp.bfloat16)
    weight_term = lax.dot_general(
        propagated, grad_pre, (((0,), (0,)), ((), ())), preferred_element_type=jnp.float32
    )
    bias_term = jnp.sum(grad_pre.astype(jnp.float32), axis=0)
    pad_rows = (-(feature_width + 1)) % 8
    packed = jnp.concatenate(
        [weight_term, bias_term[None, :], jnp.zeros((pad_rows, feature_width), jnp.float32)], axis=0
    )
    packed = reduce_all(packed)
    weight_grad = packed[:feature_width]
    bias_grad = packed[feature_width]
    return (layer_out, weight_grad, bias_grad)


def solution(mesh):
    flat = P(ALL_AXES, None)
    placed = (
        flat,
        P(),
        P(),
        P(ROW_AXES, None, None, None, None),
        P(ROW_AXES, None, None),
        P(ROW_AXES, None, None),
        P(ROW_AXES, None),
        flat,
    )
    return jax.shard_map(
        shards,
        mesh=physical_mesh(mesh),
        in_specs=placed,
        out_specs=(flat, P(), P()),
        check_vma=False,
    )
```

```python
import jax
import jax.numpy as jnp
from jax import lax
from jax.sharding import Mesh
from jax.sharding import PartitionSpec as P

ROW_AXES = ("y_hi", "x", "z")
REP_AXES = ("y_lo", "core")
ALL_AXES = ROW_AXES + REP_AXES


def physical_mesh(mesh):
    rows, rep = mesh.devices.shape
    y_hi, x, y_lo = 4, 4, 2
    return Mesh(mesh.devices.reshape(y_hi, x, rows // (y_hi * x), y_lo, rep // y_lo), ALL_AXES)


def ring_gather(piece, axis):
    n = lax.axis_size(axis)
    fwd = [(i, (i + 1) % n) for i in range(n)]
    bwd = [(i, (i - 1) % n) for i in range(n)]
    pieces = {0: piece}
    left = piece
    right = piece
    for k in range(1, n // 2 + 1):
        left = lax.ppermute(left, axis, fwd)
        pieces[-k] = left
        if k < n - k:
            right = lax.ppermute(right, axis, bwd)
            pieces[k] = right
    return jnp.stack([pieces[d] for d in range(-(n // 2), n - n // 2)])


def row_coords(c):
    coords = {}
    for a in reversed(ROW_AXES):
        size = lax.axis_size(a)
        coords[a] = c % size
        c = c // size
    return coords


def plane_blocks(features, cols, across="x", within=("y_hi", "z")):
    n_across = lax.axis_size(across)
    peer_cols = {
        s: lax.ppermute(cols, across, [(i, (i - s) % n_across) for i in range(n_across)])
        for s in range(1, n_across)
    }
    stack = features
    for a in within:
        stack = ring_gather(stack, a)
    plane = stack.reshape(-1, features.shape[0], features.shape[1])

    def in_plane(c):
        coords = row_coords(c)
        flat = jnp.zeros_like(c)
        for a in reversed(within):
            size = lax.axis_size(a)
            flat = flat * size + (coords[a] - lax.axis_index(a) + size // 2) % size
        return flat

    copies = [jnp.take(plane, in_plane(cols), axis=0)]
    for s in range(1, n_across):
        sent = jnp.take(plane, in_plane(peer_cols[s]), axis=0)
        copies.append(lax.ppermute(sent, across, [(i, (i + s) % n_across) for i in range(n_across)]))
    source = (lax.axis_index(across) - row_coords(cols)[across]) % n_across
    picked = copies[0]
    for s in range(1, n_across):
        picked = jnp.where((source == s)[:, None, None], copies[s], picked)
    return picked


def halving_steps(axes):
    steps = []
    for a in axes:
        n = lax.axis_size(a)
        for b in reversed(range(n.bit_length() - 1)):
            steps.append((a, b, [(i, i ^ (1 << b)) for i in range(n)]))
    return steps


def reduce_scatter_flat(flat, steps):
    for a, b, perm in steps:
        upper = (lax.axis_index(a) >> b) & 1
        half = flat.shape[0] // 2
        lower_half, upper_half = flat[:half], flat[half:]
        send = jnp.where(upper == 1, lower_half, upper_half)
        keep = jnp.where(upper == 1, upper_half, lower_half)
        flat = keep + lax.ppermute(send, a, perm)
    return flat


def all_gather_flat(flat, steps):
    for a, b, perm in reversed(steps):
        upper = (lax.axis_index(a) >> b) & 1
        other = lax.ppermute(flat, a, perm)
        flat = jnp.where(
            upper == 1, jnp.concatenate([other, flat]), jnp.concatenate([flat, other])
        )
    return flat


def reduce_all(packed):
    rep_steps = halving_steps(("core", "y_lo"))
    flat = reduce_scatter_flat(packed.reshape(-1), rep_steps)
    for a, b, perm in halving_steps(ROW_AXES[::-1]):
        flat = flat + lax.ppermute(flat, a, perm)
    flat = all_gather_flat(flat, rep_steps)
    return flat.reshape(packed.shape)


def reduce_over_rep(partial_value):
    rows, width = partial_value.shape
    blocks = partial_value.reshape(lax.axis_size("y_lo"), lax.axis_size("core"), -1)
    core = lax.axis_index("core")
    send = jnp.where(core == 1, blocks[:, 0], blocks[:, 1])
    keep = jnp.where(core == 1, blocks[:, 1], blocks[:, 0])
    pairs = keep + lax.ppermute(send, "core", [(0, 1), (1, 0)])
    y_lo = lax.axis_index("y_lo")
    send = jnp.where(y_lo == 1, pairs[0], pairs[1])
    keep = jnp.where(y_lo == 1, pairs[1], pairs[0])
    own = keep + lax.ppermute(send, "y_lo", [(0, 1), (1, 0)])
    return own.reshape(rows // lax.axis_size(REP_AXES), width)


def shards(features, weight, bias_terms, tile_data, tile_row, tile_col, tile_count, grad_out):
    block_size = tile_data.shape[-1]
    feature_width = features.shape[1]
    row_count = lax.axis_size(REP_AXES)
    rep_index = lax.axis_index(REP_AXES)
    own_tiles = lax.dynamic_index_in_dim(tile_data[0], rep_index, 0, keepdims=False)
    own_rows = lax.dynamic_index_in_dim(tile_row[0], rep_index, 0, keepdims=False)
    own_cols = lax.dynamic_index_in_dim(tile_col[0], rep_index, 0, keepdims=False)
    own_count = lax.dynamic_index_in_dim(tile_count[0], rep_index, 0, keepdims=False)
    capacity = own_rows.shape[0]
    picked = plane_blocks(features, own_cols)
    product = jnp.einsum("tij,tjf->tif", own_tiles, picked, preferred_element_type=jnp.float32)
    live = jnp.arange(capacity, dtype=jnp.int32) < own_count
    local_ids = jnp.arange(row_count, dtype=jnp.int32)
    select = ((own_rows[None, :] == local_ids[:, None]) & live[None, :]).astype(jnp.float32)
    partial_value = jnp.einsum("bt,tif->bif", select, product)
    partial_value = partial_value.reshape(row_count * block_size, feature_width)
    propagated = reduce_over_rep(partial_value).astype(jnp.bfloat16)
    preact = jnp.dot(propagated, weight, preferred_element_type=jnp.float32) + bias_terms
    sigma = jax.nn.sigmoid(preact)
    layer_out = (preact * sigma).astype(jnp.bfloat16)
    slope = sigma * (1.0 + preact * (1.0 - sigma))
    grad_pre = (grad_out.astype(jnp.float32) * slope).astype(jnp.bfloat16)
    weight_term = lax.dot_general(
        propagated, grad_pre, (((0,), (0,)), ((), ())), preferred_element_type=jnp.float32
    )
    bias_term = jnp.sum(grad_pre.astype(jnp.float32), axis=0)
    pad_rows = (-(feature_width + 1)) % 8
    packed = jnp.concatenate(
        [weight_term, bias_term[None, :], jnp.zeros((pad_rows, feature_width), jnp.float32)], axis=0
    )
    half = feature_width // 2
    packed = jnp.concatenate([reduce_all(packed[:, :half]), reduce_all(packed[:, half:])], axis=1)
    weight_grad = packed[:feature_width]
    bias_grad = packed[feature_width]
    return (layer_out, weight_grad, bias_grad)


def solution(mesh):
    flat = P(ALL_AXES, None)
    placed = (
        flat,
        P(),
        P(),
        P(ROW_AXES, None, None, None, None),
        P(ROW_AXES, None, None),
        P(ROW_AXES, None, None),
        P(ROW_AXES, None),
        flat,
    )
    return jax.shard_map(
        shards,
        mesh=physical_mesh(mesh),
        in_specs=placed,
        out_specs=(flat, P(), P()),
        check_vma=False,
    )
```

```python
import jax
import jax.numpy as jnp
from jax import lax
from jax.sharding import Mesh
from jax.sharding import PartitionSpec as P

ROW_AXES = ("y_hi", "x", "z")
REP_AXES = ("y_lo", "core")
ALL_AXES = ROW_AXES + REP_AXES


def physical_mesh(mesh):
    rows, rep = mesh.devices.shape
    y_hi, x, y_lo = 4, 4, 2
    return Mesh(mesh.devices.reshape(y_hi, x, rows // (y_hi * x), y_lo, rep // y_lo), ALL_AXES)


def ring_gather(piece, axis):
    n = lax.axis_size(axis)
    fwd = [(i, (i + 1) % n) for i in range(n)]
    bwd = [(i, (i - 1) % n) for i in range(n)]
    pieces = {0: piece}
    left = piece
    right = piece
    for k in range(1, n // 2 + 1):
        left = lax.ppermute(left, axis, fwd)
        pieces[-k] = left
        if k < n - k:
            right = lax.ppermute(right, axis, bwd)
            pieces[k] = right
    return jnp.stack([pieces[d] for d in range(-(n // 2), n - n // 2)])


def row_coords(c):
    coords = {}
    for a in reversed(ROW_AXES):
        size = lax.axis_size(a)
        coords[a] = c % size
        c = c // size
    return coords


def plane_blocks(features, cols, across="x", within=("y_hi", "z")):
    n_across = lax.axis_size(across)
    peer_cols = {
        s: lax.ppermute(cols, across, [(i, (i - s) % n_across) for i in range(n_across)])
        for s in range(1, n_across)
    }
    stack = features
    for a in within:
        stack = ring_gather(stack, a)
    plane = stack.reshape(-1, features.shape[0], features.shape[1])

    def in_plane(c):
        coords = row_coords(c)
        flat = jnp.zeros_like(c)
        for a in reversed(within):
            size = lax.axis_size(a)
            flat = flat * size + (coords[a] - lax.axis_index(a) + size // 2) % size
        return flat

    copies = [jnp.take(plane, in_plane(cols), axis=0, mode="clip")]
    for s in range(1, n_across):
        sent = jnp.take(plane, in_plane(peer_cols[s]), axis=0, mode="clip")
        copies.append(lax.ppermute(sent, across, [(i, (i + s) % n_across) for i in range(n_across)]))
    source = (lax.axis_index(across) - row_coords(cols)[across]) % n_across
    picked = copies[0]
    for s in range(1, n_across):
        picked = jnp.where((source == s)[:, None, None], copies[s], picked)
    return picked


def halving_steps(axes):
    steps = []
    for a in axes:
        n = lax.axis_size(a)
        for b in reversed(range(n.bit_length() - 1)):
            steps.append((a, b, [(i, i ^ (1 << b)) for i in range(n)]))
    return steps


def reduce_scatter_flat(flat, steps):
    for a, b, perm in steps:
        upper = (lax.axis_index(a) >> b) & 1
        half = flat.shape[0] // 2
        lower_half, upper_half = flat[:half], flat[half:]
        send = jnp.where(upper == 1, lower_half, upper_half)
        keep = jnp.where(upper == 1, upper_half, lower_half)
        flat = keep + lax.ppermute(send, a, perm)
    return flat


def all_gather_flat(flat, steps):
    for a, b, perm in reversed(steps):
        upper = (lax.axis_index(a) >> b) & 1
        other = lax.ppermute(flat, a, perm)
        flat = jnp.where(
            upper == 1, jnp.concatenate([other, flat]), jnp.concatenate([flat, other])
        )
    return flat


def reduce_all(packed):
    rep_steps = halving_steps(("core", "y_lo"))
    flat = reduce_scatter_flat(packed.reshape(-1), rep_steps)
    for a, b, perm in halving_steps(ROW_AXES[::-1]):
        flat = flat + lax.ppermute(flat, a, perm)
    flat = all_gather_flat(flat, rep_steps)
    return flat.reshape(packed.shape)


def reduce_over_rep(partial_value):
    rows, width = partial_value.shape
    blocks = partial_value.reshape(lax.axis_size("y_lo"), lax.axis_size("core"), -1)
    core = lax.axis_index("core")
    send = jnp.where(core == 1, blocks[:, 0], blocks[:, 1])
    keep = jnp.where(core == 1, blocks[:, 1], blocks[:, 0])
    pairs = keep + lax.ppermute(send, "core", [(0, 1), (1, 0)])
    y_lo = lax.axis_index("y_lo")
    send = jnp.where(y_lo == 1, pairs[0], pairs[1])
    keep = jnp.where(y_lo == 1, pairs[1], pairs[0])
    own = keep + lax.ppermute(send, "y_lo", [(0, 1), (1, 0)])
    return own.reshape(rows // lax.axis_size(REP_AXES), width)


def shards(features, weight, bias_terms, tile_data, tile_row, tile_col, tile_count, grad_out):
    block_size = tile_data.shape[-1]
    feature_width = features.shape[1]
    row_count = lax.axis_size(REP_AXES)
    rep_index = lax.axis_index(REP_AXES)
    own_tiles = lax.dynamic_index_in_dim(tile_data[0], rep_index, 0, keepdims=False)
    own_rows = lax.dynamic_index_in_dim(tile_row[0], rep_index, 0, keepdims=False)
    own_cols = lax.dynamic_index_in_dim(tile_col[0], rep_index, 0, keepdims=False)
    own_count = lax.dynamic_index_in_dim(tile_count[0], rep_index, 0, keepdims=False)
    capacity = own_rows.shape[0]
    picked = plane_blocks(features, own_cols)
    product = jnp.einsum("tij,tjf->tif", own_tiles, picked, preferred_element_type=jnp.float32)
    live = jnp.arange(capacity, dtype=jnp.int32) < own_count
    local_ids = jnp.arange(row_count, dtype=jnp.int32)
    select = ((own_rows[None, :] == local_ids[:, None]) & live[None, :]).astype(jnp.float32)
    partial_value = jnp.einsum("bt,tif->bif", select, product)
    partial_value = partial_value.reshape(row_count * block_size, feature_width)
    propagated = reduce_over_rep(partial_value).astype(jnp.bfloat16)
    preact = jnp.dot(propagated, weight, preferred_element_type=jnp.float32) + bias_terms
    sigma = jax.nn.sigmoid(preact)
    layer_out = (preact * sigma).astype(jnp.bfloat16)
    slope = sigma * (1.0 + preact * (1.0 - sigma))
    grad_pre = (grad_out.astype(jnp.float32) * slope).astype(jnp.bfloat16)
    weight_term = lax.dot_general(
        propagated, grad_pre, (((0,), (0,)), ((), ())), preferred_element_type=jnp.float32
    )
    bias_term = jnp.sum(grad_pre.astype(jnp.float32), axis=0)
    pad_rows = (-(feature_width + 1)) % 8
    packed = jnp.concatenate(
        [weight_term, bias_term[None, :], jnp.zeros((pad_rows, feature_width), jnp.float32)], axis=0
    )
    packed = reduce_all(packed)
    weight_grad = packed[:feature_width]
    bias_grad = packed[feature_width]
    return (layer_out, weight_grad, bias_grad)


def solution(mesh):
    flat = P(ALL_AXES, None)
    placed = (
        flat,
        P(),
        P(),
        P(ROW_AXES, None, None, None, None),
        P(ROW_AXES, None, None),
        P(ROW_AXES, None, None),
        P(ROW_AXES, None),
        flat,
    )
    return jax.shard_map(
        shards,
        mesh=physical_mesh(mesh),
        in_specs=placed,
        out_specs=(flat, P(), P()),
        check_vma=False,
    )
```

```python
import jax
import jax.numpy as jnp
from jax import lax
from jax.sharding import Mesh
from jax.sharding import PartitionSpec as P

ROW_AXES = ("y_hi", "x", "z")
REP_AXES = ("y_lo", "core")
ALL_AXES = ROW_AXES + REP_AXES


def physical_mesh(mesh):
    rows, rep = mesh.devices.shape
    y_hi, x, y_lo = 4, 4, 2
    return Mesh(mesh.devices.reshape(y_hi, x, rows // (y_hi * x), y_lo, rep // y_lo), ALL_AXES)


def ring_gather(piece, axis):
    n = lax.axis_size(axis)
    fwd = [(i, (i + 1) % n) for i in range(n)]
    bwd = [(i, (i - 1) % n) for i in range(n)]
    pieces = {0: piece}
    left = piece
    right = piece
    for k in range(1, n // 2 + 1):
        left = lax.ppermute(left, axis, fwd)
        pieces[-k] = left
        if k < n - k:
            right = lax.ppermute(right, axis, bwd)
            pieces[k] = right
    return jnp.stack([pieces[d] for d in range(-(n // 2), n - n // 2)])


def row_coords(c):
    coords = {}
    for a in reversed(ROW_AXES):
        size = lax.axis_size(a)
        coords[a] = c % size
        c = c // size
    return coords


def plane_blocks(features, cols, across="x", within=("y_hi", "z")):
    n_across = lax.axis_size(across)
    peer_cols = {
        s: lax.ppermute(cols, across, [(i, (i - s) % n_across) for i in range(n_across)])
        for s in range(1, n_across)
    }
    stack = features
    for a in within:
        stack = ring_gather(stack, a)
    plane = stack.reshape(-1, features.shape[0], features.shape[1])

    def in_plane(c):
        coords = row_coords(c)
        flat = jnp.zeros_like(c)
        for a in reversed(within):
            size = lax.axis_size(a)
            flat = flat * size + (coords[a] - lax.axis_index(a) + size // 2) % size
        return flat

    copies = [jnp.take(plane, in_plane(cols), axis=0, mode="clip")]
    for s in range(1, n_across):
        sent = jnp.take(plane, in_plane(peer_cols[s]), axis=0, mode="clip")
        copies.append(lax.ppermute(sent, across, [(i, (i + s) % n_across) for i in range(n_across)]))
    source = (lax.axis_index(across) - row_coords(cols)[across]) % n_across
    picked = copies[0]
    for s in range(1, n_across):
        picked = jnp.where((source == s)[:, None, None], copies[s], picked)
    return picked


def halving_steps(axes):
    steps = []
    for a in axes:
        n = lax.axis_size(a)
        for b in reversed(range(n.bit_length() - 1)):
            steps.append((a, b, [(i, i ^ (1 << b)) for i in range(n)]))
    return steps


def reduce_scatter_flat(flat, steps):
    for a, b, perm in steps:
        upper = (lax.axis_index(a) >> b) & 1
        half = flat.shape[0] // 2
        lower_half, upper_half = flat[:half], flat[half:]
        send = jnp.where(upper == 1, lower_half, upper_half)
        keep = jnp.where(upper == 1, upper_half, lower_half)
        flat = keep + lax.ppermute(send, a, perm)
    return flat


def all_gather_flat(flat, steps):
    for a, b, perm in reversed(steps):
        upper = (lax.axis_index(a) >> b) & 1
        other = lax.ppermute(flat, a, perm)
        flat = jnp.where(
            upper == 1, jnp.concatenate([other, flat]), jnp.concatenate([flat, other])
        )
    return flat


def reduce_all(packed):
    rep_steps = halving_steps(("core", "y_lo"))
    flat = reduce_scatter_flat(packed.reshape(-1), rep_steps)
    for a, b, perm in halving_steps(ROW_AXES[::-1]):
        flat = flat + lax.ppermute(flat, a, perm)
    flat = all_gather_flat(flat, rep_steps)
    return flat.reshape(packed.shape)


def reduce_over_rep(partial_value):
    rows, width = partial_value.shape
    blocks = partial_value.reshape(lax.axis_size("y_lo"), lax.axis_size("core"), -1)
    core = lax.axis_index("core")
    send = jnp.where(core == 1, blocks[:, 0], blocks[:, 1])
    keep = jnp.where(core == 1, blocks[:, 1], blocks[:, 0])
    pairs = keep + lax.ppermute(send, "core", [(0, 1), (1, 0)])
    y_lo = lax.axis_index("y_lo")
    send = jnp.where(y_lo == 1, pairs[0], pairs[1])
    keep = jnp.where(y_lo == 1, pairs[1], pairs[0])
    own = keep + lax.ppermute(send, "y_lo", [(0, 1), (1, 0)])
    return own.reshape(rows // lax.axis_size(REP_AXES), width)


def swap(x, axis):
    return lax.ppermute(x, axis, [(0, 1), (1, 0)])


def gather_over_rep(block):
    other = swap(block, "core")
    pair = jnp.where(
        lax.axis_index("core") == 1, jnp.stack([other, block]), jnp.stack([block, other])
    )
    other = swap(pair, "y_lo")
    quad = jnp.where(
        lax.axis_index("y_lo") == 1, jnp.concatenate([other, pair]), jnp.concatenate([pair, other])
    )
    return quad.reshape(-1, *block.shape[1:])


def sum_over_rep(value):
    value = value + swap(value, "core")
    return value + swap(value, "y_lo")


def shards(features, weight, bias_terms, tile_data, tile_row, tile_col, tile_count, grad_out):
    block_size = tile_data.shape[-1]
    feature_width = features.shape[1]
    row_count = lax.axis_size(REP_AXES)
    rep_index = lax.axis_index(REP_AXES)
    own_tiles = lax.dynamic_index_in_dim(tile_data[0], rep_index, 0, keepdims=False)
    own_rows = lax.dynamic_index_in_dim(tile_row[0], rep_index, 0, keepdims=False)
    own_cols = lax.dynamic_index_in_dim(tile_col[0], rep_index, 0, keepdims=False)
    own_count = lax.dynamic_index_in_dim(tile_count[0], rep_index, 0, keepdims=False)
    capacity = own_rows.shape[0]
    picked = plane_blocks(features, own_cols)
    product = jnp.einsum("tij,tjf->tif", own_tiles, picked, preferred_element_type=jnp.float32)
    live = jnp.arange(capacity, dtype=jnp.int32) < own_count
    local_ids = jnp.arange(row_count, dtype=jnp.int32)
    select = ((own_rows[None, :] == local_ids[:, None]) & live[None, :]).astype(jnp.float32)
    partial_value = jnp.einsum("bt,tif->bif", select, product)
    partial_value = partial_value.reshape(row_count * block_size, feature_width)
    propagated = sum_over_rep(partial_value).astype(jnp.bfloat16)
    group_grad_out = gather_over_rep(grad_out)
    preact = jnp.dot(propagated, weight, preferred_element_type=jnp.float32) + bias_terms
    sigma = jax.nn.sigmoid(preact)
    layer_out = (preact * sigma).astype(jnp.bfloat16)
    layer_out = lax.dynamic_slice_in_dim(layer_out, rep_index * block_size, block_size, 0)
    slope = sigma * (1.0 + preact * (1.0 - sigma))
    grad_pre = (group_grad_out.astype(jnp.float32) * slope).astype(jnp.bfloat16)
    weight_term = lax.dot_general(
        propagated, grad_pre, (((0,), (0,)), ((), ())), preferred_element_type=jnp.float32
    )
    bias_term = jnp.sum(grad_pre.astype(jnp.float32), axis=0)
    pad_rows = (-(feature_width + 1)) % 8
    packed = jnp.concatenate(
        [weight_term, bias_term[None, :], jnp.zeros((pad_rows, feature_width), jnp.float32)], axis=0
    )
    rep_steps = halving_steps(("core", "y_lo"))
    quarter = lax.axis_index("core") * lax.axis_size("y_lo") + lax.axis_index("y_lo")
    flat = lax.dynamic_index_in_dim(packed.reshape(row_count, -1), quarter, 0, keepdims=False)
    for a, b, perm in halving_steps(ROW_AXES[::-1]):
        flat = flat + lax.ppermute(flat, a, perm)
    packed = all_gather_flat(flat, rep_steps).reshape(packed.shape)
    weight_grad = packed[:feature_width]
    bias_grad = packed[feature_width]
    return (layer_out, weight_grad, bias_grad)


def solution(mesh):
    flat = P(ALL_AXES, None)
    placed = (
        flat,
        P(),
        P(),
        P(ROW_AXES, None, None, None, None),
        P(ROW_AXES, None, None),
        P(ROW_AXES, None, None),
        P(ROW_AXES, None),
        flat,
    )
    return jax.shard_map(
        shards,
        mesh=physical_mesh(mesh),
        in_specs=placed,
        out_specs=(flat, P(), P()),
        check_vma=False,
    )
```

```python
import jax
import jax.numpy as jnp
from jax import lax
from jax.sharding import Mesh
from jax.sharding import PartitionSpec as P

ROW_AXES = ("y_hi", "x", "z")
REP_AXES = ("y_lo", "core")
ALL_AXES = ROW_AXES + REP_AXES


def physical_mesh(mesh):
    rows, rep = mesh.devices.shape
    y_hi, x, y_lo = 4, 4, 2
    return Mesh(mesh.devices.reshape(y_hi, x, rows // (y_hi * x), y_lo, rep // y_lo), ALL_AXES)


def ring_gather(piece, axis):
    n = lax.axis_size(axis)
    fwd = [(i, (i + 1) % n) for i in range(n)]
    bwd = [(i, (i - 1) % n) for i in range(n)]
    pieces = {0: piece}
    left = piece
    right = piece
    for k in range(1, n // 2 + 1):
        left = lax.ppermute(left, axis, fwd)
        pieces[-k] = left
        if k < n - k:
            right = lax.ppermute(right, axis, bwd)
            pieces[k] = right
    return jnp.stack([pieces[d] for d in range(-(n // 2), n - n // 2)])


def row_coords(c):
    coords = {}
    for a in reversed(ROW_AXES):
        size = lax.axis_size(a)
        coords[a] = c % size
        c = c // size
    return coords


def plane_blocks(features, cols, across="x", within=("y_hi", "z")):
    n_across = lax.axis_size(across)
    peer_cols = {
        s: lax.ppermute(cols, across, [(i, (i - s) % n_across) for i in range(n_across)])
        for s in range(1, n_across)
    }
    stack = features
    for a in within:
        stack = ring_gather(stack, a)
    plane = stack.reshape(-1, features.shape[0], features.shape[1])

    def in_plane(c):
        coords = row_coords(c)
        flat = jnp.zeros_like(c)
        for a in reversed(within):
            size = lax.axis_size(a)
            flat = flat * size + (coords[a] - lax.axis_index(a) + size // 2) % size
        return flat

    copies = [jnp.take(plane, in_plane(cols), axis=0, mode="clip")]
    for s in range(1, n_across):
        sent = jnp.take(plane, in_plane(peer_cols[s]), axis=0, mode="clip")
        copies.append(lax.ppermute(sent, across, [(i, (i + s) % n_across) for i in range(n_across)]))
    source = (lax.axis_index(across) - row_coords(cols)[across]) % n_across
    picked = copies[0]
    for s in range(1, n_across):
        picked = jnp.where((source == s)[:, None, None], copies[s], picked)
    return picked


def halving_steps(axes):
    steps = []
    for a in axes:
        n = lax.axis_size(a)
        for b in reversed(range(n.bit_length() - 1)):
            steps.append((a, b, [(i, i ^ (1 << b)) for i in range(n)]))
    return steps


def doubling_steps(axes):
    steps = []
    for a in axes:
        n = lax.axis_size(a)
        for b in range(n.bit_length() - 2):
            steps.append((a, [(i, i ^ (1 << b)) for i in range(n)]))
        steps.append((a, [(i, n - 1 - i) for i in range(n)]))
    return steps


def reduce_scatter_flat(flat, steps):
    for a, b, perm in steps:
        upper = (lax.axis_index(a) >> b) & 1
        half = flat.shape[0] // 2
        lower_half, upper_half = flat[:half], flat[half:]
        send = jnp.where(upper == 1, lower_half, upper_half)
        keep = jnp.where(upper == 1, upper_half, lower_half)
        flat = keep + lax.ppermute(send, a, perm)
    return flat


def all_gather_flat(flat, steps):
    for a, b, perm in reversed(steps):
        upper = (lax.axis_index(a) >> b) & 1
        other = lax.ppermute(flat, a, perm)
        flat = jnp.where(
            upper == 1, jnp.concatenate([other, flat]), jnp.concatenate([flat, other])
        )
    return flat


def reduce_all(packed):
    rep_steps = halving_steps(("core", "y_lo"))
    flat = reduce_scatter_flat(packed.reshape(-1), rep_steps)
    for a, b, perm in halving_steps(ROW_AXES[::-1]):
        flat = flat + lax.ppermute(flat, a, perm)
    flat = all_gather_flat(flat, rep_steps)
    return flat.reshape(packed.shape)


def reduce_over_rep(partial_value):
    rows, width = partial_value.shape
    blocks = partial_value.reshape(lax.axis_size("y_lo"), lax.axis_size("core"), -1)
    core = lax.axis_index("core")
    send = jnp.where(core == 1, blocks[:, 0], blocks[:, 1])
    keep = jnp.where(core == 1, blocks[:, 1], blocks[:, 0])
    pairs = keep + lax.ppermute(send, "core", [(0, 1), (1, 0)])
    y_lo = lax.axis_index("y_lo")
    send = jnp.where(y_lo == 1, pairs[0], pairs[1])
    keep = jnp.where(y_lo == 1, pairs[1], pairs[0])
    own = keep + lax.ppermute(send, "y_lo", [(0, 1), (1, 0)])
    return own.reshape(rows // lax.axis_size(REP_AXES), width)


def swap(x, axis):
    return lax.ppermute(x, axis, [(0, 1), (1, 0)])


def gather_over_rep(block):
    other = swap(block, "core")
    pair = jnp.where(
        lax.axis_index("core") == 1, jnp.stack([other, block]), jnp.stack([block, other])
    )
    other = swap(pair, "y_lo")
    quad = jnp.where(
        lax.axis_index("y_lo") == 1, jnp.concatenate([other, pair]), jnp.concatenate([pair, other])
    )
    return quad.reshape(-1, *block.shape[1:])


def sum_over_rep(value):
    value = value + swap(value, "core")
    return value + swap(value, "y_lo")


def shards(features, weight, bias_terms, tile_data, tile_row, tile_col, tile_count, grad_out):
    block_size = tile_data.shape[-1]
    feature_width = features.shape[1]
    row_count = lax.axis_size(REP_AXES)
    rep_index = lax.axis_index(REP_AXES)
    own_tiles = lax.dynamic_index_in_dim(tile_data[0], rep_index, 0, keepdims=False)
    own_rows = lax.dynamic_index_in_dim(tile_row[0], rep_index, 0, keepdims=False)
    own_cols = lax.dynamic_index_in_dim(tile_col[0], rep_index, 0, keepdims=False)
    own_count = lax.dynamic_index_in_dim(tile_count[0], rep_index, 0, keepdims=False)
    capacity = own_rows.shape[0]
    picked = plane_blocks(features, own_cols)
    product = jnp.einsum("tij,tjf->tif", own_tiles, picked, preferred_element_type=jnp.float32)
    live = jnp.arange(capacity, dtype=jnp.int32) < own_count
    local_ids = jnp.arange(row_count, dtype=jnp.int32)
    select = ((own_rows[None, :] == local_ids[:, None]) & live[None, :]).astype(jnp.float32)
    partial_value = jnp.einsum("bt,tif->bif", select, product)
    partial_value = partial_value.reshape(row_count * block_size, feature_width)
    propagated = sum_over_rep(partial_value).astype(jnp.bfloat16)
    group_grad_out = gather_over_rep(grad_out)
    preact = jnp.dot(propagated, weight, preferred_element_type=jnp.float32) + bias_terms
    sigma = jax.nn.sigmoid(preact)
    layer_out = (preact * sigma).astype(jnp.bfloat16)
    layer_out = lax.dynamic_slice_in_dim(layer_out, rep_index * block_size, block_size, 0)
    slope = sigma * (1.0 + preact * (1.0 - sigma))
    grad_pre = (group_grad_out.astype(jnp.float32) * slope).astype(jnp.bfloat16)
    weight_term = lax.dot_general(
        propagated, grad_pre, (((0,), (0,)), ((), ())), preferred_element_type=jnp.float32
    )
    bias_term = jnp.sum(grad_pre.astype(jnp.float32), axis=0)
    pad_rows = (-(feature_width + 1)) % 8
    packed = jnp.concatenate(
        [weight_term, bias_term[None, :], jnp.zeros((pad_rows, feature_width), jnp.float32)], axis=0
    )
    rep_steps = halving_steps(("core", "y_lo"))
    quarter = lax.axis_index("core") * lax.axis_size("y_lo") + lax.axis_index("y_lo")
    flat = lax.dynamic_index_in_dim(packed.reshape(row_count, -1), quarter, 0, keepdims=False)
    for a, perm in doubling_steps(ROW_AXES[::-1]):
        flat = flat + lax.ppermute(flat, a, perm)
    packed = all_gather_flat(flat, rep_steps).reshape(packed.shape)
    weight_grad = packed[:feature_width]
    bias_grad = packed[feature_width]
    return (layer_out, weight_grad, bias_grad)


def solution(mesh):
    flat = P(ALL_AXES, None)
    placed = (
        flat,
        P(),
        P(),
        P(ROW_AXES, None, None, None, None),
        P(ROW_AXES, None, None),
        P(ROW_AXES, None, None),
        P(ROW_AXES, None),
        flat,
    )
    return jax.shard_map(
        shards,
        mesh=physical_mesh(mesh),
        in_specs=placed,
        out_specs=(flat, P(), P()),
        check_vma=False,
    )
```

```python
import jax
import jax.numpy as jnp
from jax import lax
from jax.sharding import Mesh
from jax.sharding import PartitionSpec as P

ROW_AXES = ("y_hi", "x", "z")
REP_AXES = ("y_lo", "core")
ALL_AXES = ROW_AXES + REP_AXES


def physical_mesh(mesh):
    rows, rep = mesh.devices.shape
    y_hi, x, y_lo = 4, 4, 2
    return Mesh(mesh.devices.reshape(y_hi, x, rows // (y_hi * x), y_lo, rep // y_lo), ALL_AXES)


def ring_gather(piece, axis):
    n = lax.axis_size(axis)
    fwd = [(i, (i + 1) % n) for i in range(n)]
    bwd = [(i, (i - 1) % n) for i in range(n)]
    pieces = {0: piece}
    left = piece
    right = piece
    for k in range(1, n // 2 + 1):
        left = lax.ppermute(left, axis, fwd)
        pieces[-k] = left
        if k < n - k:
            right = lax.ppermute(right, axis, bwd)
            pieces[k] = right
    return jnp.stack([pieces[d] for d in range(-(n // 2), n - n // 2)])


def row_coords(c):
    coords = {}
    for a in reversed(ROW_AXES):
        size = lax.axis_size(a)
        coords[a] = c % size
        c = c // size
    return coords


def plane_blocks(features, cols, extra, across="x", within=("y_hi", "z")):
    n_across = lax.axis_size(across)
    peer_cols = {
        s: lax.ppermute(cols, across, [(i, (i - s) % n_across) for i in range(n_across)])
        for s in range(1, n_across)
    }
    stack = ring_gather(features, within[0])
    stack, peer_cols, extra = lax.optimization_barrier((stack, peer_cols, extra))
    for a in within[1:]:
        stack = ring_gather(stack, a)
    plane = stack.reshape(-1, features.shape[0], features.shape[1])

    def in_plane(c):
        coords = row_coords(c)
        flat = jnp.zeros_like(c)
        for a in reversed(within):
            size = lax.axis_size(a)
            flat = flat * size + (coords[a] - lax.axis_index(a) + size // 2) % size
        return flat

    copies = [jnp.take(plane, in_plane(cols), axis=0, mode="clip")]
    for s in range(1, n_across):
        sent = jnp.take(plane, in_plane(peer_cols[s]), axis=0, mode="clip")
        copies.append(lax.ppermute(sent, across, [(i, (i + s) % n_across) for i in range(n_across)]))
    source = (lax.axis_index(across) - row_coords(cols)[across]) % n_across
    picked = copies[0]
    for s in range(1, n_across):
        picked = jnp.where((source == s)[:, None, None], copies[s], picked)
    return picked, extra


def halving_steps(axes):
    steps = []
    for a in axes:
        n = lax.axis_size(a)
        for b in reversed(range(n.bit_length() - 1)):
            steps.append((a, b, [(i, i ^ (1 << b)) for i in range(n)]))
    return steps


def doubling_steps(axes):
    steps = []
    for a in axes:
        n = lax.axis_size(a)
        for b in range(n.bit_length() - 2):
            steps.append((a, [(i, i ^ (1 << b)) for i in range(n)]))
        steps.append((a, [(i, n - 1 - i) for i in range(n)]))
    return steps


def reduce_scatter_flat(flat, steps):
    for a, b, perm in steps:
        upper = (lax.axis_index(a) >> b) & 1
        half = flat.shape[0] // 2
        lower_half, upper_half = flat[:half], flat[half:]
        send = jnp.where(upper == 1, lower_half, upper_half)
        keep = jnp.where(upper == 1, upper_half, lower_half)
        flat = keep + lax.ppermute(send, a, perm)
    return flat


def all_gather_flat(flat, steps):
    for a, b, perm in reversed(steps):
        upper = (lax.axis_index(a) >> b) & 1
        other = lax.ppermute(flat, a, perm)
        flat = jnp.where(
            upper == 1, jnp.concatenate([other, flat]), jnp.concatenate([flat, other])
        )
    return flat


def reduce_all(packed):
    rep_steps = halving_steps(("core", "y_lo"))
    flat = reduce_scatter_flat(packed.reshape(-1), rep_steps)
    for a, b, perm in halving_steps(ROW_AXES[::-1]):
        flat = flat + lax.ppermute(flat, a, perm)
    flat = all_gather_flat(flat, rep_steps)
    return flat.reshape(packed.shape)


def reduce_over_rep(partial_value):
    rows, width = partial_value.shape
    blocks = partial_value.reshape(lax.axis_size("y_lo"), lax.axis_size("core"), -1)
    core = lax.axis_index("core")
    send = jnp.where(core == 1, blocks[:, 0], blocks[:, 1])
    keep = jnp.where(core == 1, blocks[:, 1], blocks[:, 0])
    pairs = keep + lax.ppermute(send, "core", [(0, 1), (1, 0)])
    y_lo = lax.axis_index("y_lo")
    send = jnp.where(y_lo == 1, pairs[0], pairs[1])
    keep = jnp.where(y_lo == 1, pairs[1], pairs[0])
    own = keep + lax.ppermute(send, "y_lo", [(0, 1), (1, 0)])
    return own.reshape(rows // lax.axis_size(REP_AXES), width)


def swap(x, axis):
    return lax.ppermute(x, axis, [(0, 1), (1, 0)])


def gather_over_rep(block):
    other = swap(block, "core")
    pair = jnp.where(
        lax.axis_index("core") == 1, jnp.stack([other, block]), jnp.stack([block, other])
    )
    other = swap(pair, "y_lo")
    quad = jnp.where(
        lax.axis_index("y_lo") == 1, jnp.concatenate([other, pair]), jnp.concatenate([pair, other])
    )
    return quad.reshape(-1, *block.shape[1:])


def sum_over_rep(value):
    value = value + swap(value, "core")
    return value + swap(value, "y_lo")


def shards(features, weight, bias_terms, tile_data, tile_row, tile_col, tile_count, grad_out):
    block_size = tile_data.shape[-1]
    feature_width = features.shape[1]
    row_count = lax.axis_size(REP_AXES)
    rep_index = lax.axis_index(REP_AXES)
    own_tiles = lax.dynamic_index_in_dim(tile_data[0], rep_index, 0, keepdims=False)
    own_rows = lax.dynamic_index_in_dim(tile_row[0], rep_index, 0, keepdims=False)
    own_cols = lax.dynamic_index_in_dim(tile_col[0], rep_index, 0, keepdims=False)
    own_count = lax.dynamic_index_in_dim(tile_count[0], rep_index, 0, keepdims=False)
    capacity = own_rows.shape[0]
    group_grad_out = gather_over_rep(grad_out)
    picked, group_grad_out = plane_blocks(features, own_cols, group_grad_out)
    product = jnp.einsum("tij,tjf->tif", own_tiles, picked, preferred_element_type=jnp.float32)
    live = jnp.arange(capacity, dtype=jnp.int32) < own_count
    local_ids = jnp.arange(row_count, dtype=jnp.int32)
    select = ((own_rows[None, :] == local_ids[:, None]) & live[None, :]).astype(jnp.float32)
    partial_value = jnp.einsum("bt,tif->bif", select, product)
    partial_value = partial_value.reshape(row_count * block_size, feature_width)
    propagated = sum_over_rep(partial_value).astype(jnp.bfloat16)
    preact = jnp.dot(propagated, weight, preferred_element_type=jnp.float32) + bias_terms
    sigma = jax.nn.sigmoid(preact)
    layer_out = (preact * sigma).astype(jnp.bfloat16)
    layer_out = lax.dynamic_slice_in_dim(layer_out, rep_index * block_size, block_size, 0)
    slope = sigma * (1.0 + preact * (1.0 - sigma))
    grad_pre = (group_grad_out.astype(jnp.float32) * slope).astype(jnp.bfloat16)
    weight_term = lax.dot_general(
        propagated, grad_pre, (((0,), (0,)), ((), ())), preferred_element_type=jnp.float32
    )
    bias_term = jnp.sum(grad_pre.astype(jnp.float32), axis=0)
    pad_rows = (-(feature_width + 1)) % 8
    packed = jnp.concatenate(
        [weight_term, bias_term[None, :], jnp.zeros((pad_rows, feature_width), jnp.float32)], axis=0
    )
    rep_steps = halving_steps(("core", "y_lo"))
    quarter = lax.axis_index("core") * lax.axis_size("y_lo") + lax.axis_index("y_lo")
    flat = lax.dynamic_index_in_dim(packed.reshape(row_count, -1), quarter, 0, keepdims=False)
    for a, perm in doubling_steps(ROW_AXES[::-1]):
        flat = flat + lax.ppermute(flat, a, perm)
    packed = all_gather_flat(flat, rep_steps).reshape(packed.shape)
    weight_grad = packed[:feature_width]
    bias_grad = packed[feature_width]
    return (layer_out, weight_grad, bias_grad)


def solution(mesh):
    flat = P(ALL_AXES, None)
    placed = (
        flat,
        P(),
        P(),
        P(ROW_AXES, None, None, None, None),
        P(ROW_AXES, None, None),
        P(ROW_AXES, None, None),
        P(ROW_AXES, None),
        flat,
    )
    return jax.shard_map(
        shards,
        mesh=physical_mesh(mesh),
        in_specs=placed,
        out_specs=(flat, P(), P()),
        check_vma=False,
    )
```

```python
import jax
import jax.numpy as jnp
from jax import lax
from jax.sharding import Mesh
from jax.sharding import PartitionSpec as P

ROW_AXES = ("y_hi", "x", "z")
REP_AXES = ("y_lo", "core")
ALL_AXES = ROW_AXES + REP_AXES


def physical_mesh(mesh):
    rows, rep = mesh.devices.shape
    y_hi, x, y_lo = 4, 4, 2
    return Mesh(mesh.devices.reshape(y_hi, x, rows // (y_hi * x), y_lo, rep // y_lo), ALL_AXES)


def round_gather(piece, axis):
    n = lax.axis_size(axis)
    pieces = []
    for k in range(n):
        d = k - n // 2
        if d == 0:
            pieces.append(piece)
        else:
            pieces.append(lax.ppermute(piece, axis, [(i, (i - d) % n) for i in range(n)]))
    return jnp.stack(pieces)


def round_sum(value, axis):
    n = lax.axis_size(axis)
    got = [value] + [
        lax.ppermute(value, axis, [(i, (i - d) % n) for i in range(n)]) for d in range(1, n)
    ]
    by_position = jnp.take(
        jnp.stack(got), (jnp.arange(n) - lax.axis_index(axis)) % n, axis=0, mode="clip"
    )
    total = by_position[0]
    for p in range(1, n):
        total = total + by_position[p]
    return total


def ring_gather(piece, axis):
    n = lax.axis_size(axis)
    fwd = [(i, (i + 1) % n) for i in range(n)]
    bwd = [(i, (i - 1) % n) for i in range(n)]
    pieces = {0: piece}
    left = piece
    right = piece
    for k in range(1, n // 2 + 1):
        left = lax.ppermute(left, axis, fwd)
        pieces[-k] = left
        if k < n - k:
            right = lax.ppermute(right, axis, bwd)
            pieces[k] = right
    return jnp.stack([pieces[d] for d in range(-(n // 2), n - n // 2)])


def row_coords(c):
    coords = {}
    for a in reversed(ROW_AXES):
        size = lax.axis_size(a)
        coords[a] = c % size
        c = c // size
    return coords


def plane_blocks(features, cols, across="x", within=("y_hi", "z")):
    n_across = lax.axis_size(across)
    peer_cols = {
        s: lax.ppermute(cols, across, [(i, (i - s) % n_across) for i in range(n_across)])
        for s in range(1, n_across)
    }
    stack = features
    for a in within:
        stack = round_gather(stack, a) if lax.axis_size(a) <= 4 else ring_gather(stack, a)
    plane = stack.reshape(-1, features.shape[0], features.shape[1])

    def in_plane(c):
        coords = row_coords(c)
        flat = jnp.zeros_like(c)
        for a in reversed(within):
            size = lax.axis_size(a)
            flat = flat * size + (coords[a] - lax.axis_index(a) + size // 2) % size
        return flat

    copies = [jnp.take(plane, in_plane(cols), axis=0, mode="clip")]
    for s in range(1, n_across):
        sent = jnp.take(plane, in_plane(peer_cols[s]), axis=0, mode="clip")
        copies.append(lax.ppermute(sent, across, [(i, (i + s) % n_across) for i in range(n_across)]))
    source = (lax.axis_index(across) - row_coords(cols)[across]) % n_across
    picked = copies[0]
    for s in range(1, n_across):
        picked = jnp.where((source == s)[:, None, None], copies[s], picked)
    return picked


def halving_steps(axes):
    steps = []
    for a in axes:
        n = lax.axis_size(a)
        for b in reversed(range(n.bit_length() - 1)):
            steps.append((a, b, [(i, i ^ (1 << b)) for i in range(n)]))
    return steps


def doubling_steps(axes):
    steps = []
    for a in axes:
        n = lax.axis_size(a)
        for b in range(n.bit_length() - 2):
            steps.append((a, [(i, i ^ (1 << b)) for i in range(n)]))
        steps.append((a, [(i, n - 1 - i) for i in range(n)]))
    return steps


def reduce_scatter_flat(flat, steps):
    for a, b, perm in steps:
        upper = (lax.axis_index(a) >> b) & 1
        half = flat.shape[0] // 2
        lower_half, upper_half = flat[:half], flat[half:]
        send = jnp.where(upper == 1, lower_half, upper_half)
        keep = jnp.where(upper == 1, upper_half, lower_half)
        flat = keep + lax.ppermute(send, a, perm)
    return flat


def all_gather_flat(flat, steps):
    for a, b, perm in reversed(steps):
        upper = (lax.axis_index(a) >> b) & 1
        other = lax.ppermute(flat, a, perm)
        flat = jnp.where(
            upper == 1, jnp.concatenate([other, flat]), jnp.concatenate([flat, other])
        )
    return flat


def reduce_all(packed):
    rep_steps = halving_steps(("core", "y_lo"))
    flat = reduce_scatter_flat(packed.reshape(-1), rep_steps)
    for a, b, perm in halving_steps(ROW_AXES[::-1]):
        flat = flat + lax.ppermute(flat, a, perm)
    flat = all_gather_flat(flat, rep_steps)
    return flat.reshape(packed.shape)


def reduce_over_rep(partial_value):
    rows, width = partial_value.shape
    blocks = partial_value.reshape(lax.axis_size("y_lo"), lax.axis_size("core"), -1)
    core = lax.axis_index("core")
    send = jnp.where(core == 1, blocks[:, 0], blocks[:, 1])
    keep = jnp.where(core == 1, blocks[:, 1], blocks[:, 0])
    pairs = keep + lax.ppermute(send, "core", [(0, 1), (1, 0)])
    y_lo = lax.axis_index("y_lo")
    send = jnp.where(y_lo == 1, pairs[0], pairs[1])
    keep = jnp.where(y_lo == 1, pairs[1], pairs[0])
    own = keep + lax.ppermute(send, "y_lo", [(0, 1), (1, 0)])
    return own.reshape(rows // lax.axis_size(REP_AXES), width)


def swap(x, axis):
    return lax.ppermute(x, axis, [(0, 1), (1, 0)])


def gather_over_rep(block):
    other = swap(block, "core")
    pair = jnp.where(
        lax.axis_index("core") == 1, jnp.stack([other, block]), jnp.stack([block, other])
    )
    other = swap(pair, "y_lo")
    quad = jnp.where(
        lax.axis_index("y_lo") == 1, jnp.concatenate([other, pair]), jnp.concatenate([pair, other])
    )
    return quad.reshape(-1, *block.shape[1:])


def sum_over_rep(value):
    value = value + swap(value, "core")
    return value + swap(value, "y_lo")


def shards(features, weight, bias_terms, tile_data, tile_row, tile_col, tile_count, grad_out):
    block_size = tile_data.shape[-1]
    feature_width = features.shape[1]
    row_count = lax.axis_size(REP_AXES)
    rep_index = lax.axis_index(REP_AXES)
    own_tiles = lax.dynamic_index_in_dim(tile_data[0], rep_index, 0, keepdims=False)
    own_rows = lax.dynamic_index_in_dim(tile_row[0], rep_index, 0, keepdims=False)
    own_cols = lax.dynamic_index_in_dim(tile_col[0], rep_index, 0, keepdims=False)
    own_count = lax.dynamic_index_in_dim(tile_count[0], rep_index, 0, keepdims=False)
    capacity = own_rows.shape[0]
    picked = plane_blocks(features, own_cols)
    product = jnp.einsum("tij,tjf->tif", own_tiles, picked, preferred_element_type=jnp.float32)
    live = jnp.arange(capacity, dtype=jnp.int32) < own_count
    local_ids = jnp.arange(row_count, dtype=jnp.int32)
    select = ((own_rows[None, :] == local_ids[:, None]) & live[None, :]).astype(jnp.float32)
    partial_value = jnp.einsum("bt,tif->bif", select, product)
    partial_value = partial_value.reshape(row_count * block_size, feature_width)
    propagated = sum_over_rep(partial_value).astype(jnp.bfloat16)
    group_grad_out = gather_over_rep(grad_out)
    preact = jnp.dot(propagated, weight, preferred_element_type=jnp.float32) + bias_terms
    sigma = jax.nn.sigmoid(preact)
    layer_out = (preact * sigma).astype(jnp.bfloat16)
    layer_out = lax.dynamic_slice_in_dim(layer_out, rep_index * block_size, block_size, 0)
    slope = sigma * (1.0 + preact * (1.0 - sigma))
    grad_pre = (group_grad_out.astype(jnp.float32) * slope).astype(jnp.bfloat16)
    weight_term = lax.dot_general(
        propagated, grad_pre, (((0,), (0,)), ((), ())), preferred_element_type=jnp.float32
    )
    bias_term = jnp.sum(grad_pre.astype(jnp.float32), axis=0)
    pad_rows = (-(feature_width + 1)) % 8
    packed = jnp.concatenate(
        [weight_term, bias_term[None, :], jnp.zeros((pad_rows, feature_width), jnp.float32)], axis=0
    )
    rep_steps = halving_steps(("core", "y_lo"))
    quarter = lax.axis_index("core") * lax.axis_size("y_lo") + lax.axis_index("y_lo")
    flat = lax.dynamic_index_in_dim(packed.reshape(row_count, -1), quarter, 0, keepdims=False)
    for a in ROW_AXES[::-1]:
        if lax.axis_size(a) <= 4:
            flat = round_sum(flat, a)
        else:
            for _, perm in doubling_steps((a,)):
                flat = flat + lax.ppermute(flat, a, perm)
    packed = all_gather_flat(flat, rep_steps).reshape(packed.shape)
    weight_grad = packed[:feature_width]
    bias_grad = packed[feature_width]
    return (layer_out, weight_grad, bias_grad)


def solution(mesh):
    flat = P(ALL_AXES, None)
    placed = (
        flat,
        P(),
        P(),
        P(ROW_AXES, None, None, None, None),
        P(ROW_AXES, None, None),
        P(ROW_AXES, None, None),
        P(ROW_AXES, None),
        flat,
    )
    return jax.shard_map(
        shards,
        mesh=physical_mesh(mesh),
        in_specs=placed,
        out_specs=(flat, P(), P()),
        check_vma=False,
    )
```

```python
import jax
import jax.numpy as jnp
from jax import lax
from jax.sharding import Mesh
from jax.sharding import PartitionSpec as P

ROW_AXES = ("y_hi", "x", "z")
REP_AXES = ("y_lo", "core")
ALL_AXES = ROW_AXES + REP_AXES


def physical_mesh(mesh):
    rows, rep = mesh.devices.shape
    y_hi, x, y_lo = 4, 4, 2
    return Mesh(mesh.devices.reshape(y_hi, x, rows // (y_hi * x), y_lo, rep // y_lo), ALL_AXES)


def round_gather(piece, axis):
    n = lax.axis_size(axis)
    pieces = []
    for k in range(n):
        d = k - n // 2
        if d == 0:
            pieces.append(piece)
        else:
            pieces.append(lax.ppermute(piece, axis, [(i, (i - d) % n) for i in range(n)]))
    return jnp.stack(pieces)


def ring_gather(piece, axis):
    n = lax.axis_size(axis)
    fwd = [(i, (i + 1) % n) for i in range(n)]
    bwd = [(i, (i - 1) % n) for i in range(n)]
    pieces = {0: piece}
    left = piece
    right = piece
    for k in range(1, n // 2 + 1):
        left = lax.ppermute(left, axis, fwd)
        pieces[-k] = left
        if k < n - k:
            right = lax.ppermute(right, axis, bwd)
            pieces[k] = right
    return jnp.stack([pieces[d] for d in range(-(n // 2), n - n // 2)])


def row_coords(c):
    coords = {}
    for a in reversed(ROW_AXES):
        size = lax.axis_size(a)
        coords[a] = c % size
        c = c // size
    return coords


def plane_blocks(features, cols, across="x", within=("y_hi", "z")):
    n_across = lax.axis_size(across)
    peer_cols = {
        s: lax.ppermute(cols, across, [(i, (i - s) % n_across) for i in range(n_across)])
        for s in range(1, n_across)
    }
    stack = features
    for a in within:
        stack = round_gather(stack, a) if lax.axis_size(a) <= 4 else ring_gather(stack, a)
    plane = stack.reshape(-1, features.shape[0], features.shape[1])

    def in_plane(c):
        coords = row_coords(c)
        flat = jnp.zeros_like(c)
        for a in reversed(within):
            size = lax.axis_size(a)
            flat = flat * size + (coords[a] - lax.axis_index(a) + size // 2) % size
        return flat

    copies = [jnp.take(plane, in_plane(cols), axis=0, mode="clip")]
    for s in range(1, n_across):
        sent = jnp.take(plane, in_plane(peer_cols[s]), axis=0, mode="clip")
        copies.append(lax.ppermute(sent, across, [(i, (i + s) % n_across) for i in range(n_across)]))
    source = (lax.axis_index(across) - row_coords(cols)[across]) % n_across
    picked = copies[0]
    for s in range(1, n_across):
        picked = jnp.where((source == s)[:, None, None], copies[s], picked)
    return picked


def halving_steps(axes):
    steps = []
    for a in axes:
        n = lax.axis_size(a)
        for b in reversed(range(n.bit_length() - 1)):
            steps.append((a, b, [(i, i ^ (1 << b)) for i in range(n)]))
    return steps


def doubling_steps(axes):
    steps = []
    for a in axes:
        n = lax.axis_size(a)
        for b in range(n.bit_length() - 2):
            steps.append((a, [(i, i ^ (1 << b)) for i in range(n)]))
        steps.append((a, [(i, n - 1 - i) for i in range(n)]))
    return steps


def reduce_scatter_flat(flat, steps):
    for a, b, perm in steps:
        upper = (lax.axis_index(a) >> b) & 1
        half = flat.shape[0] // 2
        lower_half, upper_half = flat[:half], flat[half:]
        send = jnp.where(upper == 1, lower_half, upper_half)
        keep = jnp.where(upper == 1, upper_half, lower_half)
        flat = keep + lax.ppermute(send, a, perm)
    return flat


def all_gather_flat(flat, steps):
    for a, b, perm in reversed(steps):
        upper = (lax.axis_index(a) >> b) & 1
        other = lax.ppermute(flat, a, perm)
        flat = jnp.where(
            upper == 1, jnp.concatenate([other, flat]), jnp.concatenate([flat, other])
        )
    return flat


def reduce_all(packed):
    rep_steps = halving_steps(("core", "y_lo"))
    flat = reduce_scatter_flat(packed.reshape(-1), rep_steps)
    for a, b, perm in halving_steps(ROW_AXES[::-1]):
        flat = flat + lax.ppermute(flat, a, perm)
    flat = all_gather_flat(flat, rep_steps)
    return flat.reshape(packed.shape)


def reduce_over_rep(partial_value):
    rows, width = partial_value.shape
    blocks = partial_value.reshape(lax.axis_size("y_lo"), lax.axis_size("core"), -1)
    core = lax.axis_index("core")
    send = jnp.where(core == 1, blocks[:, 0], blocks[:, 1])
    keep = jnp.where(core == 1, blocks[:, 1], blocks[:, 0])
    pairs = keep + lax.ppermute(send, "core", [(0, 1), (1, 0)])
    y_lo = lax.axis_index("y_lo")
    send = jnp.where(y_lo == 1, pairs[0], pairs[1])
    keep = jnp.where(y_lo == 1, pairs[1], pairs[0])
    own = keep + lax.ppermute(send, "y_lo", [(0, 1), (1, 0)])
    return own.reshape(rows // lax.axis_size(REP_AXES), width)


def swap(x, axis):
    return lax.ppermute(x, axis, [(0, 1), (1, 0)])


def gather_over_rep(block):
    other = swap(block, "core")
    pair = jnp.where(
        lax.axis_index("core") == 1, jnp.stack([other, block]), jnp.stack([block, other])
    )
    other = swap(pair, "y_lo")
    quad = jnp.where(
        lax.axis_index("y_lo") == 1, jnp.concatenate([other, pair]), jnp.concatenate([pair, other])
    )
    return quad.reshape(-1, *block.shape[1:])


def sum_over_rep(value):
    value = value + swap(value, "core")
    return value + swap(value, "y_lo")


def shards(features, weight, bias_terms, tile_data, tile_row, tile_col, tile_count, grad_out):
    block_size = tile_data.shape[-1]
    feature_width = features.shape[1]
    row_count = lax.axis_size(REP_AXES)
    rep_index = lax.axis_index(REP_AXES)
    own_tiles = lax.dynamic_index_in_dim(tile_data[0], rep_index, 0, keepdims=False)
    own_rows = lax.dynamic_index_in_dim(tile_row[0], rep_index, 0, keepdims=False)
    own_cols = lax.dynamic_index_in_dim(tile_col[0], rep_index, 0, keepdims=False)
    own_count = lax.dynamic_index_in_dim(tile_count[0], rep_index, 0, keepdims=False)
    capacity = own_rows.shape[0]
    picked = plane_blocks(features, own_cols)
    product = jnp.einsum("tij,tjf->tif", own_tiles, picked, preferred_element_type=jnp.float32)
    live = jnp.arange(capacity, dtype=jnp.int32) < own_count
    local_ids = jnp.arange(row_count, dtype=jnp.int32)
    select = ((own_rows[None, :] == local_ids[:, None]) & live[None, :]).astype(jnp.float32)
    partial_value = jnp.einsum("bt,tif->bif", select, product)
    partial_value = partial_value.reshape(row_count * block_size, feature_width)
    propagated = sum_over_rep(partial_value).astype(jnp.bfloat16)
    group_grad_out = gather_over_rep(grad_out)
    preact = jnp.dot(propagated, weight, preferred_element_type=jnp.float32) + bias_terms
    sigma = jax.nn.sigmoid(preact)
    layer_out = (preact * sigma).astype(jnp.bfloat16)
    layer_out = lax.dynamic_slice_in_dim(layer_out, rep_index * block_size, block_size, 0)
    slope = sigma * (1.0 + preact * (1.0 - sigma))
    grad_pre = (group_grad_out.astype(jnp.float32) * slope).astype(jnp.bfloat16)
    weight_term = lax.dot_general(
        propagated, grad_pre, (((0,), (0,)), ((), ())), preferred_element_type=jnp.float32
    )
    bias_term = jnp.sum(grad_pre.astype(jnp.float32), axis=0)
    pad_rows = (-(feature_width + 1)) % 8
    packed = jnp.concatenate(
        [weight_term, bias_term[None, :], jnp.zeros((pad_rows, feature_width), jnp.float32)], axis=0
    )
    rep_steps = halving_steps(("core", "y_lo"))
    quarter = lax.axis_index("core") * lax.axis_size("y_lo") + lax.axis_index("y_lo")
    flat = lax.dynamic_index_in_dim(packed.reshape(row_count, -1), quarter, 0, keepdims=False)
    for a, perm in doubling_steps(ROW_AXES[::-1]):
        flat = flat + lax.ppermute(flat, a, perm)
    packed = all_gather_flat(flat, rep_steps).reshape(packed.shape)
    weight_grad = packed[:feature_width]
    bias_grad = packed[feature_width]
    return (layer_out, weight_grad, bias_grad)


def solution(mesh):
    flat = P(ALL_AXES, None)
    placed = (
        flat,
        P(),
        P(),
        P(ROW_AXES, None, None, None, None),
        P(ROW_AXES, None, None),
        P(ROW_AXES, None, None),
        P(ROW_AXES, None),
        flat,
    )
    return jax.shard_map(
        shards,
        mesh=physical_mesh(mesh),
        in_specs=placed,
        out_specs=(flat, P(), P()),
        check_vma=False,
    )
```

```python
import jax
import jax.numpy as jnp
from jax import lax
from jax.sharding import Mesh
from jax.sharding import PartitionSpec as P

ROW_AXES = ("y_hi", "x", "z")
REP_AXES = ("y_lo", "core")
ALL_AXES = ROW_AXES + REP_AXES


def physical_mesh(mesh):
    rows, rep = mesh.devices.shape
    y_hi, x, y_lo = 4, 4, 2
    return Mesh(mesh.devices.reshape(y_hi, x, rows // (y_hi * x), y_lo, rep // y_lo), ALL_AXES)


def round_gather(piece, axis):
    n = lax.axis_size(axis)
    pieces = []
    for k in range(n):
        d = k - n // 2
        if d == 0:
            pieces.append(piece)
        else:
            pieces.append(lax.ppermute(piece, axis, [(i, (i - d) % n) for i in range(n)]))
    return jnp.stack(pieces)


def doubling_gather(piece, axis):
    n = lax.axis_size(axis)
    idx = lax.axis_index(axis)
    stack = piece[None]
    for b in range(n.bit_length() - 1):
        if (1 << b) < n // 2:
            perm = [(i, i ^ (1 << b)) for i in range(n)]
            later = ((idx >> b) & 1) == 1
        else:
            perm = [(i, n - 1 - i) for i in range(n)]
            later = idx >= n // 2
        other = lax.ppermute(stack, axis, perm)
        stack = jnp.where(later, jnp.concatenate([other, stack]), jnp.concatenate([stack, other]))
    return stack


def ring_gather(piece, axis):
    n = lax.axis_size(axis)
    fwd = [(i, (i + 1) % n) for i in range(n)]
    bwd = [(i, (i - 1) % n) for i in range(n)]
    pieces = {0: piece}
    left = piece
    right = piece
    for k in range(1, n // 2 + 1):
        left = lax.ppermute(left, axis, fwd)
        pieces[-k] = left
        if k < n - k:
            right = lax.ppermute(right, axis, bwd)
            pieces[k] = right
    return jnp.stack([pieces[d] for d in range(-(n // 2), n - n // 2)])


def row_coords(c):
    coords = {}
    for a in reversed(ROW_AXES):
        size = lax.axis_size(a)
        coords[a] = c % size
        c = c // size
    return coords


def plane_blocks(features, cols, across="x", within=("y_hi", "z")):
    n_across = lax.axis_size(across)
    peer_cols = {
        s: lax.ppermute(cols, across, [(i, (i - s) % n_across) for i in range(n_across)])
        for s in range(1, n_across)
    }
    stack = features
    for a in within:
        stack = round_gather(stack, a) if lax.axis_size(a) <= 4 else doubling_gather(stack, a)
    plane = stack.reshape(-1, features.shape[0], features.shape[1])

    def in_plane(c):
        coords = row_coords(c)
        flat = jnp.zeros_like(c)
        for a in reversed(within):
            size = lax.axis_size(a)
            if size <= 4:
                k = (coords[a] - lax.axis_index(a) + size // 2) % size
            else:
                k = coords[a]
            flat = flat * size + k
        return flat

    copies = [jnp.take(plane, in_plane(cols), axis=0, mode="clip")]
    for s in range(1, n_across):
        sent = jnp.take(plane, in_plane(peer_cols[s]), axis=0, mode="clip")
        copies.append(lax.ppermute(sent, across, [(i, (i + s) % n_across) for i in range(n_across)]))
    source = (lax.axis_index(across) - row_coords(cols)[across]) % n_across
    picked = copies[0]
    for s in range(1, n_across):
        picked = jnp.where((source == s)[:, None, None], copies[s], picked)
    return picked


def halving_steps(axes):
    steps = []
    for a in axes:
        n = lax.axis_size(a)
        for b in reversed(range(n.bit_length() - 1)):
            steps.append((a, b, [(i, i ^ (1 << b)) for i in range(n)]))
    return steps


def doubling_steps(axes):
    steps = []
    for a in axes:
        n = lax.axis_size(a)
        for b in range(n.bit_length() - 2):
            steps.append((a, [(i, i ^ (1 << b)) for i in range(n)]))
        steps.append((a, [(i, n - 1 - i) for i in range(n)]))
    return steps


def reduce_scatter_flat(flat, steps):
    for a, b, perm in steps:
        upper = (lax.axis_index(a) >> b) & 1
        half = flat.shape[0] // 2
        lower_half, upper_half = flat[:half], flat[half:]
        send = jnp.where(upper == 1, lower_half, upper_half)
        keep = jnp.where(upper == 1, upper_half, lower_half)
        flat = keep + lax.ppermute(send, a, perm)
    return flat


def all_gather_flat(flat, steps):
    for a, b, perm in reversed(steps):
        upper = (lax.axis_index(a) >> b) & 1
        other = lax.ppermute(flat, a, perm)
        flat = jnp.where(
            upper == 1, jnp.concatenate([other, flat]), jnp.concatenate([flat, other])
        )
    return flat


def reduce_all(packed):
    rep_steps = halving_steps(("core", "y_lo"))
    flat = reduce_scatter_flat(packed.reshape(-1), rep_steps)
    for a, b, perm in halving_steps(ROW_AXES[::-1]):
        flat = flat + lax.ppermute(flat, a, perm)
    flat = all_gather_flat(flat, rep_steps)
    return flat.reshape(packed.shape)


def reduce_over_rep(partial_value):
    rows, width = partial_value.shape
    blocks = partial_value.reshape(lax.axis_size("y_lo"), lax.axis_size("core"), -1)
    core = lax.axis_index("core")
    send = jnp.where(core == 1, blocks[:, 0], blocks[:, 1])
    keep = jnp.where(core == 1, blocks[:, 1], blocks[:, 0])
    pairs = keep + lax.ppermute(send, "core", [(0, 1), (1, 0)])
    y_lo = lax.axis_index("y_lo")
    send = jnp.where(y_lo == 1, pairs[0], pairs[1])
    keep = jnp.where(y_lo == 1, pairs[1], pairs[0])
    own = keep + lax.ppermute(send, "y_lo", [(0, 1), (1, 0)])
    return own.reshape(rows // lax.axis_size(REP_AXES), width)


def swap(x, axis):
    return lax.ppermute(x, axis, [(0, 1), (1, 0)])


def gather_over_rep(block):
    other = swap(block, "core")
    pair = jnp.where(
        lax.axis_index("core") == 1, jnp.stack([other, block]), jnp.stack([block, other])
    )
    other = swap(pair, "y_lo")
    quad = jnp.where(
        lax.axis_index("y_lo") == 1, jnp.concatenate([other, pair]), jnp.concatenate([pair, other])
    )
    return quad.reshape(-1, *block.shape[1:])


def sum_over_rep(value):
    value = value + swap(value, "core")
    return value + swap(value, "y_lo")


def shards(features, weight, bias_terms, tile_data, tile_row, tile_col, tile_count, grad_out):
    block_size = tile_data.shape[-1]
    feature_width = features.shape[1]
    row_count = lax.axis_size(REP_AXES)
    rep_index = lax.axis_index(REP_AXES)
    own_tiles = lax.dynamic_index_in_dim(tile_data[0], rep_index, 0, keepdims=False)
    own_rows = lax.dynamic_index_in_dim(tile_row[0], rep_index, 0, keepdims=False)
    own_cols = lax.dynamic_index_in_dim(tile_col[0], rep_index, 0, keepdims=False)
    own_count = lax.dynamic_index_in_dim(tile_count[0], rep_index, 0, keepdims=False)
    capacity = own_rows.shape[0]
    picked = plane_blocks(features, own_cols)
    product = jnp.einsum("tij,tjf->tif", own_tiles, picked, preferred_element_type=jnp.float32)
    live = jnp.arange(capacity, dtype=jnp.int32) < own_count
    local_ids = jnp.arange(row_count, dtype=jnp.int32)
    select = ((own_rows[None, :] == local_ids[:, None]) & live[None, :]).astype(jnp.float32)
    partial_value = jnp.einsum("bt,tif->bif", select, product)
    partial_value = partial_value.reshape(row_count * block_size, feature_width)
    propagated = sum_over_rep(partial_value).astype(jnp.bfloat16)
    group_grad_out = gather_over_rep(grad_out)
    preact = jnp.dot(propagated, weight, preferred_element_type=jnp.float32) + bias_terms
    sigma = jax.nn.sigmoid(preact)
    layer_out = (preact * sigma).astype(jnp.bfloat16)
    layer_out = lax.dynamic_slice_in_dim(layer_out, rep_index * block_size, block_size, 0)
    slope = sigma * (1.0 + preact * (1.0 - sigma))
    grad_pre = (group_grad_out.astype(jnp.float32) * slope).astype(jnp.bfloat16)
    weight_term = lax.dot_general(
        propagated, grad_pre, (((0,), (0,)), ((), ())), preferred_element_type=jnp.float32
    )
    bias_term = jnp.sum(grad_pre.astype(jnp.float32), axis=0)
    pad_rows = (-(feature_width + 1)) % 8
    packed = jnp.concatenate(
        [weight_term, bias_term[None, :], jnp.zeros((pad_rows, feature_width), jnp.float32)], axis=0
    )
    rep_steps = halving_steps(("core", "y_lo"))
    quarter = lax.axis_index("core") * lax.axis_size("y_lo") + lax.axis_index("y_lo")
    flat = lax.dynamic_index_in_dim(packed.reshape(row_count, -1), quarter, 0, keepdims=False)
    for a, perm in doubling_steps(ROW_AXES[::-1]):
        flat = flat + lax.ppermute(flat, a, perm)
    packed = all_gather_flat(flat, rep_steps).reshape(packed.shape)
    weight_grad = packed[:feature_width]
    bias_grad = packed[feature_width]
    return (layer_out, weight_grad, bias_grad)


def solution(mesh):
    flat = P(ALL_AXES, None)
    placed = (
        flat,
        P(),
        P(),
        P(ROW_AXES, None, None, None, None),
        P(ROW_AXES, None, None),
        P(ROW_AXES, None, None),
        P(ROW_AXES, None),
        flat,
    )
    return jax.shard_map(
        shards,
        mesh=physical_mesh(mesh),
        in_specs=placed,
        out_specs=(flat, P(), P()),
        check_vma=False,
    )
```

```python
import jax
import jax.numpy as jnp
from jax import lax
from jax.sharding import Mesh
from jax.sharding import PartitionSpec as P

ROW_AXES = ("y_hi", "x", "z")
REP_AXES = ("y_lo", "core")
ALL_AXES = ROW_AXES + REP_AXES


def physical_mesh(mesh):
    rows, rep = mesh.devices.shape
    y_hi, x, y_lo = 4, 4, 2
    return Mesh(mesh.devices.reshape(y_hi, x, rows // (y_hi * x), y_lo, rep // y_lo), ALL_AXES)


def round_gather(piece, axis):
    n = lax.axis_size(axis)
    pieces = []
    for k in range(n):
        d = k - n // 2
        if d == 0:
            pieces.append(piece)
        else:
            pieces.append(lax.ppermute(piece, axis, [(i, (i - d) % n) for i in range(n)]))
    return jnp.stack(pieces)


def ring_gather(piece, axis):
    n = lax.axis_size(axis)
    fwd = [(i, (i + 1) % n) for i in range(n)]
    bwd = [(i, (i - 1) % n) for i in range(n)]
    pieces = {0: piece}
    left = piece
    right = piece
    for k in range(1, n // 2 + 1):
        left = lax.ppermute(left, axis, fwd)
        pieces[-k] = left
        if k < n - k:
            right = lax.ppermute(right, axis, bwd)
            pieces[k] = right
    return jnp.stack([pieces[d] for d in range(-(n // 2), n - n // 2)])


def row_coords(c):
    coords = {}
    for a in reversed(ROW_AXES):
        size = lax.axis_size(a)
        coords[a] = c % size
        c = c // size
    return coords


def plane_blocks(features, cols, extra, across="x", within=("y_hi", "z")):
    n_across = lax.axis_size(across)
    peer_cols = {
        s: lax.ppermute(cols, across, [(i, (i - s) % n_across) for i in range(n_across)])
        for s in range(1, n_across)
    }
    stack = features
    for a in within:
        stack = round_gather(stack, a) if lax.axis_size(a) <= 4 else ring_gather(stack, a)
    plane = stack.reshape(-1, features.shape[0], features.shape[1])

    def in_plane(c):
        coords = row_coords(c)
        flat = jnp.zeros_like(c)
        for a in reversed(within):
            size = lax.axis_size(a)
            flat = flat * size + (coords[a] - lax.axis_index(a) + size // 2) % size
        return flat

    copies = [jnp.take(plane, in_plane(cols), axis=0, mode="clip")]
    for s in range(1, n_across):
        sent = jnp.take(plane, in_plane(peer_cols[s]), axis=0, mode="clip")
        copies.append(lax.ppermute(sent, across, [(i, (i + s) % n_across) for i in range(n_across)]))
    copies, extra = lax.optimization_barrier((copies, extra))
    source = (lax.axis_index(across) - row_coords(cols)[across]) % n_across
    picked = copies[0]
    for s in range(1, n_across):
        picked = jnp.where((source == s)[:, None, None], copies[s], picked)
    return picked, extra


def halving_steps(axes):
    steps = []
    for a in axes:
        n = lax.axis_size(a)
        for b in reversed(range(n.bit_length() - 1)):
            steps.append((a, b, [(i, i ^ (1 << b)) for i in range(n)]))
    return steps


def doubling_steps(axes):
    steps = []
    for a in axes:
        n = lax.axis_size(a)
        for b in range(n.bit_length() - 2):
            steps.append((a, [(i, i ^ (1 << b)) for i in range(n)]))
        steps.append((a, [(i, n - 1 - i) for i in range(n)]))
    return steps


def reduce_scatter_flat(flat, steps):
    for a, b, perm in steps:
        upper = (lax.axis_index(a) >> b) & 1
        half = flat.shape[0] // 2
        lower_half, upper_half = flat[:half], flat[half:]
        send = jnp.where(upper == 1, lower_half, upper_half)
        keep = jnp.where(upper == 1, upper_half, lower_half)
        flat = keep + lax.ppermute(send, a, perm)
    return flat


def all_gather_flat(flat, steps):
    for a, b, perm in reversed(steps):
        upper = (lax.axis_index(a) >> b) & 1
        other = lax.ppermute(flat, a, perm)
        flat = jnp.where(
            upper == 1, jnp.concatenate([other, flat]), jnp.concatenate([flat, other])
        )
    return flat


def reduce_all(packed):
    rep_steps = halving_steps(("core", "y_lo"))
    flat = reduce_scatter_flat(packed.reshape(-1), rep_steps)
    for a, b, perm in halving_steps(ROW_AXES[::-1]):
        flat = flat + lax.ppermute(flat, a, perm)
    flat = all_gather_flat(flat, rep_steps)
    return flat.reshape(packed.shape)


def reduce_over_rep(partial_value):
    rows, width = partial_value.shape
    blocks = partial_value.reshape(lax.axis_size("y_lo"), lax.axis_size("core"), -1)
    core = lax.axis_index("core")
    send = jnp.where(core == 1, blocks[:, 0], blocks[:, 1])
    keep = jnp.where(core == 1, blocks[:, 1], blocks[:, 0])
    pairs = keep + lax.ppermute(send, "core", [(0, 1), (1, 0)])
    y_lo = lax.axis_index("y_lo")
    send = jnp.where(y_lo == 1, pairs[0], pairs[1])
    keep = jnp.where(y_lo == 1, pairs[1], pairs[0])
    own = keep + lax.ppermute(send, "y_lo", [(0, 1), (1, 0)])
    return own.reshape(rows // lax.axis_size(REP_AXES), width)


def swap(x, axis):
    return lax.ppermute(x, axis, [(0, 1), (1, 0)])


def gather_over_rep(block):
    other = swap(block, "core")
    pair = jnp.where(
        lax.axis_index("core") == 1, jnp.stack([other, block]), jnp.stack([block, other])
    )
    other = swap(pair, "y_lo")
    quad = jnp.where(
        lax.axis_index("y_lo") == 1, jnp.concatenate([other, pair]), jnp.concatenate([pair, other])
    )
    return quad.reshape(-1, *block.shape[1:])


def sum_over_rep(value):
    value = value + swap(value, "core")
    return value + swap(value, "y_lo")


def shards(features, weight, bias_terms, tile_data, tile_row, tile_col, tile_count, grad_out):
    block_size = tile_data.shape[-1]
    feature_width = features.shape[1]
    row_count = lax.axis_size(REP_AXES)
    rep_index = lax.axis_index(REP_AXES)
    own_tiles = lax.dynamic_index_in_dim(tile_data[0], rep_index, 0, keepdims=False)
    own_rows = lax.dynamic_index_in_dim(tile_row[0], rep_index, 0, keepdims=False)
    own_cols = lax.dynamic_index_in_dim(tile_col[0], rep_index, 0, keepdims=False)
    own_count = lax.dynamic_index_in_dim(tile_count[0], rep_index, 0, keepdims=False)
    capacity = own_rows.shape[0]
    picked, group_grad_out = plane_blocks(features, own_cols, gather_over_rep(grad_out))
    product = jnp.einsum("tij,tjf->tif", own_tiles, picked, preferred_element_type=jnp.float32)
    live = jnp.arange(capacity, dtype=jnp.int32) < own_count
    local_ids = jnp.arange(row_count, dtype=jnp.int32)
    select = ((own_rows[None, :] == local_ids[:, None]) & live[None, :]).astype(jnp.float32)
    partial_value = jnp.einsum("bt,tif->bif", select, product)
    partial_value = partial_value.reshape(row_count * block_size, feature_width)
    propagated = sum_over_rep(partial_value).astype(jnp.bfloat16)
    preact = jnp.dot(propagated, weight, preferred_element_type=jnp.float32) + bias_terms
    sigma = jax.nn.sigmoid(preact)
    layer_out = (preact * sigma).astype(jnp.bfloat16)
    layer_out = lax.dynamic_slice_in_dim(layer_out, rep_index * block_size, block_size, 0)
    slope = sigma * (1.0 + preact * (1.0 - sigma))
    grad_pre = (group_grad_out.astype(jnp.float32) * slope).astype(jnp.bfloat16)
    weight_term = lax.dot_general(
        propagated, grad_pre, (((0,), (0,)), ((), ())), preferred_element_type=jnp.float32
    )
    bias_term = jnp.sum(grad_pre.astype(jnp.float32), axis=0)
    pad_rows = (-(feature_width + 1)) % 8
    packed = jnp.concatenate(
        [weight_term, bias_term[None, :], jnp.zeros((pad_rows, feature_width), jnp.float32)], axis=0
    )
    rep_steps = halving_steps(("core", "y_lo"))
    quarter = lax.axis_index("core") * lax.axis_size("y_lo") + lax.axis_index("y_lo")
    flat = lax.dynamic_index_in_dim(packed.reshape(row_count, -1), quarter, 0, keepdims=False)
    for a, perm in doubling_steps(ROW_AXES[::-1]):
        flat = flat + lax.ppermute(flat, a, perm)
    packed = all_gather_flat(flat, rep_steps).reshape(packed.shape)
    weight_grad = packed[:feature_width]
    bias_grad = packed[feature_width]
    return (layer_out, weight_grad, bias_grad)


def solution(mesh):
    flat = P(ALL_AXES, None)
    placed = (
        flat,
        P(),
        P(),
        P(ROW_AXES, None, None, None, None),
        P(ROW_AXES, None, None),
        P(ROW_AXES, None, None),
        P(ROW_AXES, None),
        flat,
    )
    return jax.shard_map(
        shards,
        mesh=physical_mesh(mesh),
        in_specs=placed,
        out_specs=(flat, P(), P()),
        check_vma=False,
    )
```

```python
import jax
import jax.numpy as jnp
from jax import lax
from jax.sharding import Mesh
from jax.sharding import PartitionSpec as P

ROW_AXES = ("y_hi", "x", "z")
REP_AXES = ("y_lo", "core")
ALL_AXES = ROW_AXES + REP_AXES


def physical_mesh(mesh):
    rows, rep = mesh.devices.shape
    y_hi, x, y_lo = 4, 4, 2
    return Mesh(mesh.devices.reshape(y_hi, x, rows // (y_hi * x), y_lo, rep // y_lo), ALL_AXES)


def round_gather(piece, axis):
    n = lax.axis_size(axis)
    pieces = []
    for k in range(n):
        d = k - n // 2
        if d == 0:
            pieces.append(piece)
        else:
            pieces.append(lax.ppermute(piece, axis, [(i, (i - d) % n) for i in range(n)]))
    return jnp.stack(pieces)


def ring_gather(piece, axis):
    n = lax.axis_size(axis)
    fwd = [(i, (i + 1) % n) for i in range(n)]
    bwd = [(i, (i - 1) % n) for i in range(n)]
    pieces = {0: piece}
    left = piece
    right = piece
    for k in range(1, n // 2 + 1):
        left = lax.ppermute(left, axis, fwd)
        pieces[-k] = left
        if k < n - k:
            right = lax.ppermute(right, axis, bwd)
            pieces[k] = right
    return jnp.stack([pieces[d] for d in range(-(n // 2), n - n // 2)])


def row_coords(c):
    coords = {}
    for a in reversed(ROW_AXES):
        size = lax.axis_size(a)
        coords[a] = c % size
        c = c // size
    return coords


def plane_blocks(features, cols, across="x", within=("z", "y_hi")):
    n_across = lax.axis_size(across)
    peer_cols = {
        s: lax.ppermute(cols, across, [(i, (i - s) % n_across) for i in range(n_across)])
        for s in range(1, n_across)
    }
    stack = features
    for a in within:
        stack = round_gather(stack, a) if lax.axis_size(a) <= 4 else ring_gather(stack, a)
    plane = stack.reshape(-1, features.shape[0], features.shape[1])

    def in_plane(c):
        coords = row_coords(c)
        flat = jnp.zeros_like(c)
        for a in reversed(within):
            size = lax.axis_size(a)
            flat = flat * size + (coords[a] - lax.axis_index(a) + size // 2) % size
        return flat

    copies = [jnp.take(plane, in_plane(cols), axis=0, mode="clip")]
    for s in range(1, n_across):
        sent = jnp.take(plane, in_plane(peer_cols[s]), axis=0, mode="clip")
        copies.append(lax.ppermute(sent, across, [(i, (i + s) % n_across) for i in range(n_across)]))
    source = (lax.axis_index(across) - row_coords(cols)[across]) % n_across
    picked = copies[0]
    for s in range(1, n_across):
        picked = jnp.where((source == s)[:, None, None], copies[s], picked)
    return picked


def halving_steps(axes):
    steps = []
    for a in axes:
        n = lax.axis_size(a)
        for b in reversed(range(n.bit_length() - 1)):
            steps.append((a, b, [(i, i ^ (1 << b)) for i in range(n)]))
    return steps


def doubling_steps(axes):
    steps = []
    for a in axes:
        n = lax.axis_size(a)
        for b in range(n.bit_length() - 2):
            steps.append((a, [(i, i ^ (1 << b)) for i in range(n)]))
        steps.append((a, [(i, n - 1 - i) for i in range(n)]))
    return steps


def reduce_scatter_flat(flat, steps):
    for a, b, perm in steps:
        upper = (lax.axis_index(a) >> b) & 1
        half = flat.shape[0] // 2
        lower_half, upper_half = flat[:half], flat[half:]
        send = jnp.where(upper == 1, lower_half, upper_half)
        keep = jnp.where(upper == 1, upper_half, lower_half)
        flat = keep + lax.ppermute(send, a, perm)
    return flat


def all_gather_flat(flat, steps):
    for a, b, perm in reversed(steps):
        upper = (lax.axis_index(a) >> b) & 1
        other = lax.ppermute(flat, a, perm)
        flat = jnp.where(
            upper == 1, jnp.concatenate([other, flat]), jnp.concatenate([flat, other])
        )
    return flat


def reduce_all(packed):
    rep_steps = halving_steps(("core", "y_lo"))
    flat = reduce_scatter_flat(packed.reshape(-1), rep_steps)
    for a, b, perm in halving_steps(ROW_AXES[::-1]):
        flat = flat + lax.ppermute(flat, a, perm)
    flat = all_gather_flat(flat, rep_steps)
    return flat.reshape(packed.shape)


def reduce_over_rep(partial_value):
    rows, width = partial_value.shape
    blocks = partial_value.reshape(lax.axis_size("y_lo"), lax.axis_size("core"), -1)
    core = lax.axis_index("core")
    send = jnp.where(core == 1, blocks[:, 0], blocks[:, 1])
    keep = jnp.where(core == 1, blocks[:, 1], blocks[:, 0])
    pairs = keep + lax.ppermute(send, "core", [(0, 1), (1, 0)])
    y_lo = lax.axis_index("y_lo")
    send = jnp.where(y_lo == 1, pairs[0], pairs[1])
    keep = jnp.where(y_lo == 1, pairs[1], pairs[0])
    own = keep + lax.ppermute(send, "y_lo", [(0, 1), (1, 0)])
    return own.reshape(rows // lax.axis_size(REP_AXES), width)


def swap(x, axis):
    return lax.ppermute(x, axis, [(0, 1), (1, 0)])


def gather_over_rep(block):
    other = swap(block, "core")
    pair = jnp.where(
        lax.axis_index("core") == 1, jnp.stack([other, block]), jnp.stack([block, other])
    )
    other = swap(pair, "y_lo")
    quad = jnp.where(
        lax.axis_index("y_lo") == 1, jnp.concatenate([other, pair]), jnp.concatenate([pair, other])
    )
    return quad.reshape(-1, *block.shape[1:])


def sum_over_rep(value):
    value = value + swap(value, "core")
    return value + swap(value, "y_lo")


def shards(features, weight, bias_terms, tile_data, tile_row, tile_col, tile_count, grad_out):
    block_size = tile_data.shape[-1]
    feature_width = features.shape[1]
    row_count = lax.axis_size(REP_AXES)
    rep_index = lax.axis_index(REP_AXES)
    own_tiles = lax.dynamic_index_in_dim(tile_data[0], rep_index, 0, keepdims=False)
    own_rows = lax.dynamic_index_in_dim(tile_row[0], rep_index, 0, keepdims=False)
    own_cols = lax.dynamic_index_in_dim(tile_col[0], rep_index, 0, keepdims=False)
    own_count = lax.dynamic_index_in_dim(tile_count[0], rep_index, 0, keepdims=False)
    capacity = own_rows.shape[0]
    picked = plane_blocks(features, own_cols)
    product = jnp.einsum("tij,tjf->tif", own_tiles, picked, preferred_element_type=jnp.float32)
    live = jnp.arange(capacity, dtype=jnp.int32) < own_count
    local_ids = jnp.arange(row_count, dtype=jnp.int32)
    select = ((own_rows[None, :] == local_ids[:, None]) & live[None, :]).astype(jnp.float32)
    partial_value = jnp.einsum("bt,tif->bif", select, product)
    partial_value = partial_value.reshape(row_count * block_size, feature_width)
    propagated = sum_over_rep(partial_value).astype(jnp.bfloat16)
    group_grad_out = gather_over_rep(grad_out)
    preact = jnp.dot(propagated, weight, preferred_element_type=jnp.float32) + bias_terms
    sigma = jax.nn.sigmoid(preact)
    layer_out = (preact * sigma).astype(jnp.bfloat16)
    layer_out = lax.dynamic_slice_in_dim(layer_out, rep_index * block_size, block_size, 0)
    slope = sigma * (1.0 + preact * (1.0 - sigma))
    grad_pre = (group_grad_out.astype(jnp.float32) * slope).astype(jnp.bfloat16)
    weight_term = lax.dot_general(
        propagated, grad_pre, (((0,), (0,)), ((), ())), preferred_element_type=jnp.float32
    )
    bias_term = jnp.sum(grad_pre.astype(jnp.float32), axis=0)
    pad_rows = (-(feature_width + 1)) % 8
    packed = jnp.concatenate(
        [weight_term, bias_term[None, :], jnp.zeros((pad_rows, feature_width), jnp.float32)], axis=0
    )
    rep_steps = halving_steps(("core", "y_lo"))
    quarter = lax.axis_index("core") * lax.axis_size("y_lo") + lax.axis_index("y_lo")
    flat = lax.dynamic_index_in_dim(packed.reshape(row_count, -1), quarter, 0, keepdims=False)
    for a, perm in doubling_steps(ROW_AXES[::-1]):
        flat = flat + lax.ppermute(flat, a, perm)
    packed = all_gather_flat(flat, rep_steps).reshape(packed.shape)
    weight_grad = packed[:feature_width]
    bias_grad = packed[feature_width]
    return (layer_out, weight_grad, bias_grad)


def solution(mesh):
    flat = P(ALL_AXES, None)
    placed = (
        flat,
        P(),
        P(),
        P(ROW_AXES, None, None, None, None),
        P(ROW_AXES, None, None),
        P(ROW_AXES, None, None),
        P(ROW_AXES, None),
        flat,
    )
    return jax.shard_map(
        shards,
        mesh=physical_mesh(mesh),
        in_specs=placed,
        out_specs=(flat, P(), P()),
        check_vma=False,
    )
```

```python
import jax
import jax.numpy as jnp
from jax import lax
from jax.sharding import Mesh
from jax.sharding import PartitionSpec as P

ROW_AXES = ("y_hi", "x", "z")
REP_AXES = ("y_lo", "core")
ALL_AXES = ROW_AXES + REP_AXES


def physical_mesh(mesh):
    rows, rep = mesh.devices.shape
    y_hi, x, y_lo = 4, 4, 2
    return Mesh(mesh.devices.reshape(y_hi, x, rows // (y_hi * x), y_lo, rep // y_lo), ALL_AXES)


def round_gather(piece, axis):
    n = lax.axis_size(axis)
    pieces = []
    for k in range(n):
        d = k - n // 2
        if d == 0:
            pieces.append(piece)
        else:
            pieces.append(lax.ppermute(piece, axis, [(i, (i - d) % n) for i in range(n)]))
    return jnp.stack(pieces)


def ring_gather(piece, axis):
    n = lax.axis_size(axis)
    fwd = [(i, (i + 1) % n) for i in range(n)]
    bwd = [(i, (i - 1) % n) for i in range(n)]
    pieces = {0: piece}
    left = piece
    right = piece
    for k in range(1, n // 2 + 1):
        left = lax.ppermute(left, axis, fwd)
        pieces[-k] = left
        if k < n - k:
            right = lax.ppermute(right, axis, bwd)
            pieces[k] = right
    return jnp.stack([pieces[d] for d in range(-(n // 2), n - n // 2)])


def row_coords(c):
    coords = {}
    for a in reversed(ROW_AXES):
        size = lax.axis_size(a)
        coords[a] = c % size
        c = c // size
    return coords


def plane_blocks(features, cols, across="x", within=("y_hi", "z")):
    n_across = lax.axis_size(across)
    peer_cols = {
        s: lax.ppermute(cols, across, [(i, (i - s) % n_across) for i in range(n_across)])
        for s in range(1, n_across)
    }
    stack = features
    for a in within:
        stack = round_gather(stack, a) if lax.axis_size(a) <= 4 else ring_gather(stack, a)
    plane = stack.reshape(-1, features.shape[0], features.shape[1])

    def in_plane(c):
        coords = row_coords(c)
        flat = jnp.zeros_like(c)
        for a in reversed(within):
            size = lax.axis_size(a)
            flat = flat * size + (coords[a] - lax.axis_index(a) + size // 2) % size
        return flat

    copies = [jnp.take(plane, in_plane(cols), axis=0, mode="clip")]
    for s in range(1, n_across):
        sent = jnp.take(plane, in_plane(peer_cols[s]), axis=0, mode="clip")
        copies.append(lax.ppermute(sent, across, [(i, (i + s) % n_across) for i in range(n_across)]))
    source = (lax.axis_index(across) - row_coords(cols)[across]) % n_across
    picked = copies[0]
    for s in range(1, n_across):
        picked = jnp.where((source == s)[:, None, None], copies[s], picked)
    return picked


def halving_steps(axes):
    steps = []
    for a in axes:
        n = lax.axis_size(a)
        for b in reversed(range(n.bit_length() - 1)):
            steps.append((a, b, [(i, i ^ (1 << b)) for i in range(n)]))
    return steps


def doubling_steps(axes):
    steps = []
    for a in axes:
        n = lax.axis_size(a)
        for b in range(n.bit_length() - 2):
            steps.append((a, [(i, i ^ (1 << b)) for i in range(n)]))
        steps.append((a, [(i, n - 1 - i) for i in range(n)]))
    return steps


def reduce_scatter_flat(flat, steps):
    for a, b, perm in steps:
        upper = (lax.axis_index(a) >> b) & 1
        half = flat.shape[0] // 2
        lower_half, upper_half = flat[:half], flat[half:]
        send = jnp.where(upper == 1, lower_half, upper_half)
        keep = jnp.where(upper == 1, upper_half, lower_half)
        flat = keep + lax.ppermute(send, a, perm)
    return flat


def all_gather_flat(flat, steps):
    for a, b, perm in reversed(steps):
        upper = (lax.axis_index(a) >> b) & 1
        other = lax.ppermute(flat, a, perm)
        flat = jnp.where(
            upper == 1, jnp.concatenate([other, flat]), jnp.concatenate([flat, other])
        )
    return flat


def reduce_all(packed):
    rep_steps = halving_steps(("core", "y_lo"))
    flat = reduce_scatter_flat(packed.reshape(-1), rep_steps)
    for a, b, perm in halving_steps(ROW_AXES[::-1]):
        flat = flat + lax.ppermute(flat, a, perm)
    flat = all_gather_flat(flat, rep_steps)
    return flat.reshape(packed.shape)


def reduce_over_rep(partial_value):
    rows, width = partial_value.shape
    blocks = partial_value.reshape(lax.axis_size("y_lo"), lax.axis_size("core"), -1)
    core = lax.axis_index("core")
    send = jnp.where(core == 1, blocks[:, 0], blocks[:, 1])
    keep = jnp.where(core == 1, blocks[:, 1], blocks[:, 0])
    pairs = keep + lax.ppermute(send, "core", [(0, 1), (1, 0)])
    y_lo = lax.axis_index("y_lo")
    send = jnp.where(y_lo == 1, pairs[0], pairs[1])
    keep = jnp.where(y_lo == 1, pairs[1], pairs[0])
    own = keep + lax.ppermute(send, "y_lo", [(0, 1), (1, 0)])
    return own.reshape(rows // lax.axis_size(REP_AXES), width)


def swap(x, axis):
    return lax.ppermute(x, axis, [(0, 1), (1, 0)])


def gather_over_rep(block):
    other = swap(block, "core")
    pair = jnp.where(
        lax.axis_index("core") == 1, jnp.stack([other, block]), jnp.stack([block, other])
    )
    other = swap(pair, "y_lo")
    quad = jnp.where(
        lax.axis_index("y_lo") == 1, jnp.concatenate([other, pair]), jnp.concatenate([pair, other])
    )
    return quad.reshape(-1, *block.shape[1:])


def sum_over_rep(value):
    value = value + swap(value, "core")
    half = value.shape[0] // 2
    other = jnp.concatenate([swap(value[:half], "y_lo"), swap(value[half:], "y_lo")])
    return value + other


def shards(features, weight, bias_terms, tile_data, tile_row, tile_col, tile_count, grad_out):
    block_size = tile_data.shape[-1]
    feature_width = features.shape[1]
    row_count = lax.axis_size(REP_AXES)
    rep_index = lax.axis_index(REP_AXES)
    own_tiles = lax.dynamic_index_in_dim(tile_data[0], rep_index, 0, keepdims=False)
    own_rows = lax.dynamic_index_in_dim(tile_row[0], rep_index, 0, keepdims=False)
    own_cols = lax.dynamic_index_in_dim(tile_col[0], rep_index, 0, keepdims=False)
    own_count = lax.dynamic_index_in_dim(tile_count[0], rep_index, 0, keepdims=False)
    capacity = own_rows.shape[0]
    picked = plane_blocks(features, own_cols)
    product = jnp.einsum("tij,tjf->tif", own_tiles, picked, preferred_element_type=jnp.float32)
    live = jnp.arange(capacity, dtype=jnp.int32) < own_count
    local_ids = jnp.arange(row_count, dtype=jnp.int32)
    select = ((own_rows[None, :] == local_ids[:, None]) & live[None, :]).astype(jnp.float32)
    partial_value = jnp.einsum("bt,tif->bif", select, product)
    partial_value = partial_value.reshape(row_count * block_size, feature_width)
    propagated = sum_over_rep(partial_value).astype(jnp.bfloat16)
    group_grad_out = gather_over_rep(grad_out)
    preact = jnp.dot(propagated, weight, preferred_element_type=jnp.float32) + bias_terms
    sigma = jax.nn.sigmoid(preact)
    layer_out = (preact * sigma).astype(jnp.bfloat16)
    layer_out = lax.dynamic_slice_in_dim(layer_out, rep_index * block_size, block_size, 0)
    slope = sigma * (1.0 + preact * (1.0 - sigma))
    grad_pre = (group_grad_out.astype(jnp.float32) * slope).astype(jnp.bfloat16)
    weight_term = lax.dot_general(
        propagated, grad_pre, (((0,), (0,)), ((), ())), preferred_element_type=jnp.float32
    )
    bias_term = jnp.sum(grad_pre.astype(jnp.float32), axis=0)
    pad_rows = (-(feature_width + 1)) % 8
    packed = jnp.concatenate(
        [weight_term, bias_term[None, :], jnp.zeros((pad_rows, feature_width), jnp.float32)], axis=0
    )
    rep_steps = halving_steps(("core", "y_lo"))
    quarter = lax.axis_index("core") * lax.axis_size("y_lo") + lax.axis_index("y_lo")
    flat = lax.dynamic_index_in_dim(packed.reshape(row_count, -1), quarter, 0, keepdims=False)
    for a, perm in doubling_steps(ROW_AXES[::-1]):
        flat = flat + lax.ppermute(flat, a, perm)
    packed = all_gather_flat(flat, rep_steps).reshape(packed.shape)
    weight_grad = packed[:feature_width]
    bias_grad = packed[feature_width]
    return (layer_out, weight_grad, bias_grad)


def solution(mesh):
    flat = P(ALL_AXES, None)
    placed = (
        flat,
        P(),
        P(),
        P(ROW_AXES, None, None, None, None),
        P(ROW_AXES, None, None),
        P(ROW_AXES, None, None),
        P(ROW_AXES, None),
        flat,
    )
    return jax.shard_map(
        shards,
        mesh=physical_mesh(mesh),
        in_specs=placed,
        out_specs=(flat, P(), P()),
        check_vma=False,
    )
```
